128 devices in a mesh: seq: 32 (over z, y, core), tp: 4 (over x).
Axes of the slice: x: 4, y: 4, z: 4, core: 2. Of those that a mesh axis runs over, the one named last changes fastest.
Arguments:
- hidden: bfloat16 [32768, 2048], P('seq', 'tp'), may hold values from -6 to 6
- x_weight: bfloat16 [2048, 4096], P(None, 'tp'), may hold values from -0.125 to 0.125
- z_weight: bfloat16 [2048, 4096], P(None, 'tp'), may hold values from -0.125 to 0.125
- bc_weight: bfloat16 [2048, 256], P(None, 'tp'), may hold values from -0.125 to 0.125
- dt_weight: bfloat16 [2048, 64], P(None, 'tp'), may hold values from -0.125 to 0.125
- conv_x: float32 [4, 4096], P(None, 'tp'), may hold values from -3 to 3
- conv_bc: float32 [4, 256], replicated, may hold values from -3 to 3
- dt_bias: float32 [64], P('tp'), may hold values from -2 to 1
- decay_rate: float32 [64], P('tp'), may hold values from 2e-05 to 0.2
- skip_gain: float32 [64], P('tp'), may hold values from 0.2 to 1.5
- norm_gain: float32 [4096], P('tp'), may hold values from 0.5 to 1.5
- out_weight: bfloat16 [4096, 2048], P('tp'), may hold values from -0.09375 to 0.09375
- lengths: int32 [4], replicated, may hold values from 1 to 16384, as said below
- owners: int32 [32], P('seq'), may hold values from 0 to 3, as said below
Outputs:
- mixed: bfloat16 [32768, 2048], P('seq', 'tp')
- final_state: float32 [32, 64, 64, 128], P('seq', 'tp')
- conv_edge_x: bfloat16 [32, 3, 4096], P('seq', None, 'tp')
- conv_edge_bc: bfloat16 [32, 3, 256], P('seq')
The draws below stay inside these ranges and needn't reach their ends.
Inputs may be any that keep to these rules, and one draw needn't show every extreme that they name: The prompts are packed in order and their lengths sum to 32768; the second prompt is the longest and holds exactly half of 32768 tokens; the third and fourth together hold at least 3 tokens, and one of them holds one or two. `owners`: every prompt is kept by the same number of indices.
All inputs are finite; a program needn't handle non-finite values.
Results may differ from the reference program's by a relative error of at most 0.013.
Values may be sent and summed in bfloat16 or wider, within the bound.
No kernel may reach another device: no remote copies, remote signals or barrier semaphores. Data moves between devices by JAX's collectives and lax.ppermute only.
A program may use at most 192 MiB of HBM per device.

```python
import math
import jax
import jax.numpy as jnp
from jax import lax

D = 2048
HEADS = 64
HDIM = 64
NS = 128
KCONV = 4
GROUP = 256
PROMPTS = 4
DIN = 4096
TOKENS = 32768
N_SEQ = 32


def draw_owners(key, part):
    order = jax.random.permutation(key, N_SEQ)
    return (order % PROMPTS).astype(jnp.int32)


def draw_lengths(key, part):
    half = TOKENS // 2
    key_first, key_short, key_slot = jax.random.split(key, 3)
    first_len = jax.random.randint(key_first, (), 1, half - KCONV + 2).astype(jnp.int32)
    short_len = jax.random.randint(key_short, (), 1, 3).astype(jnp.int32)
    other_len = (half - first_len - short_len).astype(jnp.int32)
    slot = jax.random.randint(key_slot, (), 0, 2).astype(jnp.int32)
    third = jnp.where(slot == 0, short_len, other_len)
    fourth = jnp.where(slot == 0, other_len, short_len)
    head = jnp.stack([first_len, jnp.asarray(half, jnp.int32), third, fourth]).astype(jnp.int32)
    filler = jnp.ones((PROMPTS - 4,), jnp.int32) if PROMPTS > 4 else jnp.zeros((0,), jnp.int32)
    return jnp.concatenate([head, filler])[:PROMPTS].astype(jnp.int32)


def levels(stream_key, dims, shards, smallest, top_value):
    def one(dim, parts):
        draws = jax.random.uniform(jax.random.fold_in(jax.random.fold_in(stream_key, 6), dim), (parts,), jnp.float32, smallest / len(shards), top_value / len(shards))
        return jnp.repeat(jnp.exp(draws), dims[dim] // parts).reshape((-1,) + (1,) * (len(dims) - dim - 1))

    loudness = one(*shards[0])
    for cut in shards[1:]:
        loudness = loudness * one(*cut)
    return loudness


def normal_values(own_key, shape, scale, most, cuts=(), held_as=jnp.bfloat16):
    array = scale * jax.random.normal(own_key, shape, jnp.float32)
    if cuts:
        array = array * levels(own_key, shape, cuts, -0.22, 0.18)
    return jnp.clip(array, -most, most).astype(held_as)


def setup_inputs(seed: int = 0) -> dict:
    key_of = jax.random.split(jax.random.key(seed), 15)
    hidden = normal_values(key_of[0], (TOKENS, D), 1.0, 6.0, ((0, 32), (1, 4)))
    x_weight = normal_values(key_of[1], (D, DIN), D ** -0.5, 0.125, ((1, 4),))
    z_weight = normal_values(key_of[2], (D, DIN), D ** -0.5, 0.125, ((1, 4),))
    bc_weight = normal_values(key_of[3], (D, 2 * NS), D ** -0.5, 0.125, ((1, 4),))
    dt_weight = normal_values(key_of[4], (D, HEADS), D ** -0.5, 0.125, ((1, 4),))
    conv_x = normal_values(key_of[5], (KCONV, DIN), KCONV ** -0.5, 3.0, ((1, 4),), jnp.float32)
    conv_bc = normal_values(key_of[6], (KCONV, 2 * NS), KCONV ** -0.5, 3.0, (), jnp.float32)
    dt_bias = jnp.clip(-2.0 + 3.0 * jax.random.uniform(key_of[7], (HEADS,), jnp.float32) ** levels(key_of[7], (HEADS,), ((0, 4),), -0.2, 0.2), -2.0, 1.0)
    decay_rate = jnp.clip(jnp.exp(math.log(0.2) - 9.2103404 * jax.random.uniform(key_of[8], (HEADS,), jnp.float32) ** levels(key_of[8], (HEADS,), ((0, 4),), -0.2, 0.2)), 1.9999999494757503e-05, 0.2)
    skip_gain = jnp.clip(0.2 + 1.3 * jax.random.uniform(key_of[9], (HEADS,), jnp.float32) ** levels(key_of[9], (HEADS,), ((0, 4),), -0.2, 0.2), 0.2, 1.5)
    norm_gain = jnp.clip(1.0 + 0.1 * jax.random.normal(key_of[10], (DIN,), jnp.float32), 0.5, 1.5)
    out_weight = normal_values(key_of[11], (DIN, D), DIN ** -0.5, 0.09375, ((0, 4),))
    lengths = draw_lengths(jax.random.fold_in(key_of[14], 71), 0)
    owners = draw_owners(jax.random.fold_in(key_of[14], 71), 0)
    return dict(hidden=hidden, x_weight=x_weight, z_weight=z_weight, bc_weight=bc_weight, dt_weight=dt_weight, conv_x=conv_x, conv_bc=conv_bc, dt_bias=dt_bias, decay_rate=decay_rate, skip_gain=skip_gain, norm_gain=norm_gain, out_weight=out_weight, lengths=lengths, owners=owners)


highest = lax.Precision.HIGHEST
epsilon = 1e-05

def segment_of(positions, prompt_end):
    counted = lax.optimization_barrier(jnp.sum((positions[:, None] >= prompt_end[None, :]).astype(jnp.int32), axis=1))
    return jnp.where(positions < 0, -1, counted).astype(jnp.int32)

def short_conv(extended, seg_ext, kernel):
    taps = kernel.shape[0]
    count = extended.shape[0] - taps + 1
    total = jnp.zeros((count, extended.shape[1]), jnp.float32)
    for offset in range(taps):
        same = (seg_ext[offset:offset + count] == seg_ext[taps - 1:]).astype(jnp.float32)
        total = total + extended[offset:offset + count].astype(jnp.float32) * kernel[offset][None, :] * same[:, None]
    return jax.nn.silu(total).astype(jnp.bfloat16)

def advance_block(state, block):
    x_blk, b_blk, c_blk, dt_blk, log_blk, seg_blk, seg_prior = block
    length = seg_blk.shape[0]
    acum = jnp.cumsum(log_blk, axis=0)
    index = jnp.arange(length, dtype=jnp.int32)
    keep = (seg_blk[:, None] == seg_blk[None, :]) & (index[:, None] >= index[None, :])
    spread = acum[:, None, :] - acum[None, :, :]
    decay = jnp.where(keep[:, :, None], jnp.exp(jnp.where(keep[:, :, None], spread, 0.0)), 0.0)
    scores = jnp.dot(c_blk, b_blk.T, precision=highest)
    mixing = scores[:, :, None] * decay * dt_blk[None, :, :]
    output = jnp.einsum('ijh,jhp->ihp', mixing, x_blk, precision=highest)
    inflow = jnp.where((seg_blk == seg_prior)[:, None], jnp.exp(acum), 0.0)
    output = output + inflow[:, :, None] * jnp.einsum('in,hpn->ihp', c_blk, state, precision=highest)
    closing = seg_blk[length - 1]
    tail = jnp.where((seg_blk == closing)[:, None], jnp.exp(acum[length - 1][None, :] - acum), 0.0) * dt_blk
    fresh = jnp.einsum('jh,jhp,jn->hpn', tail, x_blk, b_blk, precision=highest)
    carry = jnp.where(closing == seg_prior, jnp.exp(acum[length - 1]), 0.0)
    return (carry[:, None, None] * state + fresh, (output, state))

def state_at(start_state, seg_prior, x_rows, b_rows, dt_rows, log_rows, seg_rows, inner, prompt):
    acum = jnp.cumsum(log_rows, axis=0)
    level = acum[inner]
    index = jnp.arange(seg_rows.shape[0], dtype=jnp.int32)
    chosen = (seg_rows == prompt) & (index <= inner)
    weight = jnp.where(chosen[:, None], jnp.exp(jnp.where(chosen[:, None], level[None, :] - acum, 0.0)), 0.0) * dt_rows
    inflow = jnp.where(seg_rows[inner] == seg_prior, jnp.exp(level), 0.0)
    return inflow[:, None, None] * start_state + jnp.einsum('jh,jhp,jn->hpn', weight, x_rows, b_rows, precision=highest)

def reference(hidden, x_weight, z_weight, bc_weight, dt_weight, conv_x, conv_bc, dt_bias, decay_rate, skip_gain, norm_gain, out_weight, lengths, owners):
    total_rows = hidden.shape[0]
    prompt_end = jnp.cumsum(lengths).astype(jnp.int32)
    prompt_start = (prompt_end - lengths).astype(jnp.int32)
    positions = jnp.arange(total_rows, dtype=jnp.int32)
    segment = segment_of(positions, prompt_end)
    x_in = jnp.dot(hidden, x_weight, preferred_element_type=jnp.float32).astype(jnp.bfloat16)
    z_in = jnp.dot(hidden, z_weight, preferred_element_type=jnp.float32).astype(jnp.bfloat16)
    bc_in = jnp.dot(hidden, bc_weight, preferred_element_type=jnp.float32).astype(jnp.bfloat16)
    dt_raw = jnp.dot(hidden, dt_weight, preferred_element_type=jnp.float32)
    joined = jnp.concatenate([x_in, bc_in], axis=1)
    extended = jnp.concatenate([jnp.zeros((KCONV - 1, joined.shape[1]), jnp.bfloat16), joined], axis=0)
    seg_ext = jnp.concatenate([jnp.full((KCONV - 1,), -1, jnp.int32), segment])
    kernel = jnp.concatenate([conv_x, conv_bc], axis=1)
    mixed_in = short_conv(extended, seg_ext, kernel)
    x_conv = mixed_in[:, :DIN].astype(jnp.float32).reshape(total_rows, HEADS, HDIM)
    b_conv = mixed_in[:, DIN:DIN + NS].astype(jnp.float32)
    c_conv = mixed_in[:, DIN + NS:].astype(jnp.float32)
    step_size = jax.nn.softplus(dt_raw + dt_bias[None, :])
    log_decay = -decay_rate[None, :] * step_size
    blocks = total_rows // GROUP
    block_first = jnp.arange(blocks, dtype=jnp.int32) * GROUP
    seg_prior = segment_of(block_first - 1, prompt_end)
    x_blocks = x_conv.reshape(blocks, GROUP, HEADS, HDIM)
    b_blocks = b_conv.reshape(blocks, GROUP, NS)
    c_blocks = c_conv.reshape(blocks, GROUP, NS)
    dt_blocks = step_size.reshape(blocks, GROUP, HEADS)
    log_blocks = log_decay.reshape(blocks, GROUP, HEADS)
    seg_blocks = segment.reshape(blocks, GROUP)
    init_state = jnp.zeros((HEADS, HDIM, NS), jnp.float32)
    packed = (x_blocks, b_blocks, c_blocks, dt_blocks, log_blocks, seg_blocks, seg_prior)
    unused, (outputs, priors) = lax.scan(advance_block, init_state, packed)
    ssm = outputs.reshape(total_rows, HEADS, HDIM) + skip_gain[None, :, None] * x_conv
    gated = ssm.reshape(total_rows, DIN) * jax.nn.silu(z_in.astype(jnp.float32))
    mean_sq = lax.optimization_barrier(jnp.sum(gated * gated, axis=1)) / DIN
    normed = (gated * lax.rsqrt(mean_sq + epsilon)[:, None] * norm_gain[None, :]).astype(jnp.bfloat16)
    mixed = jnp.dot(normed, out_weight, preferred_element_type=jnp.float32).astype(jnp.bfloat16)
    last_row = prompt_end - 1
    finals = []
    edges = []
    for prompt in range(PROMPTS):
        row = last_row[prompt]
        block_id = row // GROUP
        inner = (row - block_id * GROUP).astype(jnp.int32)
        finals.append(state_at(priors[block_id], seg_prior[block_id], x_blocks[block_id], b_blocks[block_id], dt_blocks[block_id], log_blocks[block_id], seg_blocks[block_id], inner, prompt))
        window = lax.dynamic_slice_in_dim(extended, (row + 1).astype(jnp.int32), KCONV - 1, 0)
        rows_global = row - (KCONV - 2) + jnp.arange(KCONV - 1, dtype=jnp.int32)
        valid = rows_global >= prompt_start[prompt]
        edges.append(jnp.where(valid[:, None], window, jnp.zeros_like(window)))
    final_all = jnp.stack(finals)
    edge_all = jnp.stack(edges)
    final_state = final_all[owners]
    edge_kept = edge_all[owners]
    return (mixed, final_state, edge_kept[:, :, :DIN], edge_kept[:, :, DIN:])
```

```python
import jax
import jax.numpy as jnp
from jax import lax
from jax.sharding import PartitionSpec as P

NS = 128
KCONV = 4
GROUP = 256
PROMPTS = 4
DIN = 4096


highest = lax.Precision.HIGHEST
epsilon = 1e-05


def passed_along(block, axis, distance):
    devices = range(lax.axis_size(axis))
    route = [(i - distance, i) for i in devices if i - distance in devices]
    return lax.ppermute(block, axis, route)


def segment_of(positions, prompt_end):
    counted = jnp.sum((positions[:, None] >= prompt_end[None, :]).astype(jnp.int32), axis=1)
    return jnp.where(positions < 0, -1, counted)


def short_conv(extended, seg_ext, kernel):
    taps = kernel.shape[0]
    count = extended.shape[0] - taps + 1
    total = jnp.zeros((count, extended.shape[1]), jnp.float32)
    for offset in range(taps):
        same = (seg_ext[offset : offset + count] == seg_ext[taps - 1 :]).astype(jnp.float32)
        total = (
            total
            + extended[offset : offset + count].astype(jnp.float32)
            * kernel[offset][None, :]
            * same[:, None]
        )
    return jax.nn.silu(total).astype(jnp.bfloat16)


def advance_block(state, block):
    x_blk, b_blk, c_blk, dt_blk, log_blk, seg_blk, seg_prior = block
    length = seg_blk.shape[0]
    acum = jnp.cumsum(log_blk, axis=0)
    index = jnp.arange(length, dtype=jnp.int32)
    keep = (seg_blk[:, None] == seg_blk[None, :]) & (index[:, None] >= index[None, :])
    spread = acum[:, None, :] - acum[None, :, :]
    decay = jnp.where(keep[:, :, None], jnp.exp(jnp.where(keep[:, :, None], spread, 0.0)), 0.0)
    scores = jnp.dot(c_blk, b_blk.T, precision=highest)
    mixing = scores[:, :, None] * decay * dt_blk[None, :, :]
    output = jnp.einsum("ijh,jhp->ihp", mixing, x_blk, precision=highest)
    inflow = jnp.where((seg_blk == seg_prior)[:, None], jnp.exp(acum), 0.0)
    output = output + inflow[:, :, None] * jnp.einsum(
        "in,hpn->ihp", c_blk, state, precision=highest
    )
    closing = seg_blk[length - 1]
    tail = (
        jnp.where((seg_blk == closing)[:, None], jnp.exp(acum[length - 1][None, :] - acum), 0.0)
        * dt_blk
    )
    fresh = jnp.einsum("jh,jhp,jn->hpn", tail, x_blk, b_blk, precision=highest)
    carry = jnp.where(closing == seg_prior, jnp.exp(acum[length - 1]), 0.0)
    return carry[:, None, None] * state + fresh, output


def state_at(start_state, seg_prior, x_rows, b_rows, dt_rows, log_rows, seg_rows, inner, prompt):
    acum = jnp.cumsum(log_rows, axis=0)
    level = acum[inner]
    index = jnp.arange(seg_rows.shape[0], dtype=jnp.int32)
    chosen = (seg_rows == prompt) & (index <= inner)
    weight = (
        jnp.where(
            chosen[:, None], jnp.exp(jnp.where(chosen[:, None], level[None, :] - acum, 0.0)), 0.0
        )
        * dt_rows
    )
    inflow = jnp.where(seg_rows[inner] == seg_prior, jnp.exp(level), 0.0)
    return inflow[:, None, None] * start_state + jnp.einsum(
        "jh,jhp,jn->hpn", weight, x_rows, b_rows, precision=highest
    )


def per_device(
    hidden,
    x_weight,
    z_weight,
    bc_weight,
    dt_weight,
    conv_x,
    conv_bc,
    dt_bias,
    decay_rate,
    skip_gain,
    norm_gain,
    out_weight,
    lengths,
    owners,
):
    rows_here = hidden.shape[0]
    width_here = x_weight.shape[1]
    heads_here = dt_bias.shape[0]
    head_width = width_here // heads_here
    seq_count = lax.axis_size("seq")
    my_index = lax.axis_index("seq")
    first_row = my_index * rows_here
    prompt_end = jnp.cumsum(lengths)
    prompt_start = prompt_end - lengths
    positions = first_row + jnp.arange(rows_here, dtype=jnp.int32)
    segment = segment_of(positions, prompt_end)
    piece = lax.all_gather(hidden, "tp", axis=1, tiled=True)
    bc_full = lax.all_gather(bc_weight, "tp", axis=1, tiled=True)

    def take(matrix):
        return jnp.dot(piece, matrix, preferred_element_type=jnp.float32)

    x_acc = take(x_weight)
    z_acc = take(z_weight)
    dt_raw = take(dt_weight)
    bc_acc = take(bc_full)
    x_in = x_acc.astype(jnp.bfloat16)
    z_in = z_acc.astype(jnp.bfloat16)
    bc_in = bc_acc.astype(jnp.bfloat16)
    joined = jnp.concatenate([x_in, bc_in], axis=1)
    earlier = passed_along(joined[rows_here - (KCONV - 1) :], "seq", 1)
    extended = jnp.concatenate([earlier, joined], axis=0)
    seg_ext = jnp.concatenate(
        [
            segment_of(
                first_row - (KCONV - 1) + jnp.arange(KCONV - 1, dtype=jnp.int32), prompt_end
            ),
            segment,
        ]
    )
    kernel = jnp.concatenate([conv_x, conv_bc], axis=1)
    mixed_in = short_conv(extended, seg_ext, kernel)
    x_conv = mixed_in[:, :width_here].astype(jnp.float32).reshape(rows_here, heads_here, head_width)
    b_conv = mixed_in[:, width_here : width_here + NS].astype(jnp.float32)
    c_conv = mixed_in[:, width_here + NS :].astype(jnp.float32)
    step_size = jax.nn.softplus(dt_raw + dt_bias[None, :])
    log_decay = -decay_rate[None, :] * step_size
    device_prior = segment_of(jnp.reshape(first_row - 1, (1,)), prompt_end)[0]
    level = jnp.cumsum(log_decay, axis=0)
    closing = segment[rows_here - 1]
    through = jnp.where(closing == device_prior, jnp.exp(level[rows_here - 1]), 0.0)
    tail = (
        jnp.where(
            (segment == closing)[:, None], jnp.exp(level[rows_here - 1][None, :] - level), 0.0
        )
        * step_size
    )
    local_end = jnp.einsum("jh,jhp,jn->hpn", tail, x_conv, b_conv, precision=highest)
    state_cols = head_width * NS
    packed_end = jnp.concatenate(
        [
            local_end.reshape(heads_here, state_cols),
            jnp.broadcast_to(through[:, None], (heads_here, 128)),
        ],
        axis=1,
    )
    gathered = lax.all_gather(packed_end, "seq")
    throughs = gathered[:, :, state_cols]
    source = jnp.arange(seq_count, dtype=jnp.int32)
    between = (source[None, :] > source[:, None]) & (source[None, :] < my_index)
    factors = jnp.where(between[:, :, None], throughs[None, :, :], 1.0)
    weights = jnp.where((source < my_index)[:, None], jnp.prod(factors, axis=1), 0.0)
    entering = jnp.sum(weights[:, :, None] * gathered[:, :, :state_cols], axis=0).reshape(
        heads_here, head_width, NS
    )

    blocks = rows_here // GROUP
    state = jnp.zeros((heads_here, head_width, NS), jnp.float32)
    pieces = []
    for blk in range(blocks):
        rows = slice(blk * GROUP, (blk + 1) * GROUP)
        seg_prior = device_prior if blk == 0 else segment[blk * GROUP - 1]
        state, output = advance_block(
            state,
            (
                x_conv[rows],
                b_conv[rows],
                c_conv[rows],
                step_size[rows],
                log_decay[rows],
                segment[rows],
                seg_prior,
            ),
        )
        pieces.append(output)
    ssm = jnp.concatenate(pieces, axis=0)
    inflow = jnp.where((segment == device_prior)[:, None], jnp.exp(level), 0.0)
    ssm = ssm + inflow[:, :, None] * jnp.einsum("in,hpn->ihp", c_conv, entering, precision=highest)
    ssm = ssm + skip_gain[None, :, None] * x_conv
    gated = ssm.reshape(rows_here, width_here) * jax.nn.silu(z_in.astype(jnp.float32))
    square_sum = lax.psum(jnp.sum(gated * gated, axis=1), "tp")
    normed = (gated * lax.rsqrt(square_sum / DIN + epsilon)[:, None] * norm_gain[None, :]).astype(
        jnp.bfloat16
    )
    mixed_cols = lax.psum_scatter(
        lax.dot_general(
            out_weight, normed, (((0,), (1,)), ((), ())), preferred_element_type=jnp.float32
        ),
        "tp",
        scatter_dimension=0,
        tiled=True,
    )
    mixed = mixed_cols.T.astype(jnp.bfloat16)
    last_row = prompt_end - 1
    holder = last_row // rows_here
    present = holder == my_index
    inner = jnp.clip(last_row - first_row, 0, rows_here - 1)

    def finish(prompt_id, inner_row):
        return state_at(
            entering,
            device_prior,
            x_conv,
            b_conv,
            step_size,
            log_decay,
            segment,
            inner_row,
            prompt_id,
        )

    finals = jax.vmap(finish)(jnp.arange(PROMPTS, dtype=jnp.int32), inner)
    finals = jnp.where(present[:, None, None, None], finals, 0.0)

    def edge_of(inner_row, start_row, end_row):
        window = lax.dynamic_slice_in_dim(extended, inner_row + 1, KCONV - 1, 0)
        rows_global = end_row - (KCONV - 2) + jnp.arange(KCONV - 1, dtype=jnp.int32)
        return jnp.where((rows_global >= start_row)[:, None], window, jnp.zeros_like(window))

    edges = jax.vmap(edge_of)(inner, prompt_start, last_row)
    edges = jnp.where(present[:, None, None], edges.astype(jnp.float32), 0.0)
    edge_cols = (KCONV - 1) * edges.shape[2]
    combined = jnp.concatenate(
        [finals.reshape(PROMPTS, heads_here * state_cols), edges.reshape(PROMPTS, edge_cols)],
        axis=1,
    )
    combined_all = lax.psum(combined, "seq")
    keeper = owners[0]
    kept = combined_all[keeper]
    final_state = kept[: heads_here * state_cols].reshape(1, heads_here, head_width, NS)
    kept_edges = kept[heads_here * state_cols :].reshape(KCONV - 1, edges.shape[2])
    conv_edge_x = kept_edges[:, :width_here].astype(jnp.bfloat16)[None]
    conv_edge_bc = kept_edges[:, width_here:].astype(jnp.bfloat16)[None]
    return (mixed, final_state, conv_edge_x, conv_edge_bc)


def solution(mesh):
    return jax.shard_map(
        per_device,
        mesh=mesh,
        in_specs=(
            P("seq", "tp"),
            P(None, "tp"),
            P(None, "tp"),
            P(None, "tp"),
            P(None, "tp"),
            P(None, "tp"),
            P(),
            P("tp"),
            P("tp"),
            P("tp"),
            P("tp"),
            P("tp", None),
            P(),
            P("seq"),
        ),
        out_specs=(
            P("seq", "tp"),
            P("seq", "tp", None, None),
            P("seq", None, "tp"),
            P("seq", None, None),
        ),
        check_vma=False,
    )
```

```python
import jax
import jax.numpy as jnp
from jax import lax
from jax.sharding import PartitionSpec as P

NS = 128
KCONV = 4
GROUP = 256
PROMPTS = 4
DIN = 4096


highest = lax.Precision.HIGHEST
epsilon = 1e-05


def passed_along(block, axis, distance):
    devices = range(lax.axis_size(axis))
    route = [(i - distance, i) for i in devices if i - distance in devices]
    return lax.ppermute(block, axis, route)


def segment_of(positions, prompt_end):
    counted = jnp.sum((positions[:, None] >= prompt_end[None, :]).astype(jnp.int32), axis=1)
    return jnp.where(positions < 0, -1, counted)


def short_conv(extended, seg_ext, kernel):
    taps = kernel.shape[0]
    count = extended.shape[0] - taps + 1
    total = jnp.zeros((count, extended.shape[1]), jnp.float32)
    for offset in range(taps):
        same = (seg_ext[offset : offset + count] == seg_ext[taps - 1 :]).astype(jnp.float32)
        total = (
            total
            + extended[offset : offset + count].astype(jnp.float32)
            * kernel[offset][None, :]
            * same[:, None]
        )
    return jax.nn.silu(total).astype(jnp.bfloat16)


def advance_block(state, block):
    x_blk, b_blk, c_blk, dt_blk, log_blk, seg_blk, seg_prior = block
    length = seg_blk.shape[0]
    acum = jnp.cumsum(log_blk, axis=0)
    index = jnp.arange(length, dtype=jnp.int32)
    keep = (seg_blk[:, None] == seg_blk[None, :]) & (index[:, None] >= index[None, :])
    spread = acum[:, None, :] - acum[None, :, :]
    decay = jnp.where(keep[:, :, None], jnp.exp(jnp.where(keep[:, :, None], spread, 0.0)), 0.0)
    scores = jnp.dot(c_blk, b_blk.T, precision=highest)
    mixing = scores[:, :, None] * decay * dt_blk[None, :, :]
    output = jnp.einsum("ijh,jhp->ihp", mixing, x_blk, precision=highest)
    inflow = jnp.where((seg_blk == seg_prior)[:, None], jnp.exp(acum), 0.0)
    output = output + inflow[:, :, None] * jnp.einsum(
        "in,hpn->ihp", c_blk, state, precision=highest
    )
    closing = seg_blk[length - 1]
    tail = (
        jnp.where((seg_blk == closing)[:, None], jnp.exp(acum[length - 1][None, :] - acum), 0.0)
        * dt_blk
    )
    fresh = jnp.einsum("jh,jhp,jn->hpn", tail, x_blk, b_blk, precision=highest)
    carry = jnp.where(closing == seg_prior, jnp.exp(acum[length - 1]), 0.0)
    return carry[:, None, None] * state + fresh, output


def state_at(start_state, seg_prior, x_rows, b_rows, dt_rows, log_rows, seg_rows, inner, prompt):
    acum = jnp.cumsum(log_rows, axis=0)
    level = acum[inner]
    index = jnp.arange(seg_rows.shape[0], dtype=jnp.int32)
    chosen = (seg_rows == prompt) & (index <= inner)
    weight = (
        jnp.where(
            chosen[:, None], jnp.exp(jnp.where(chosen[:, None], level[None, :] - acum, 0.0)), 0.0
        )
        * dt_rows
    )
    inflow = jnp.where(seg_rows[inner] == seg_prior, jnp.exp(level), 0.0)
    return inflow[:, None, None] * start_state + jnp.einsum(
        "jh,jhp,jn->hpn", weight, x_rows, b_rows, precision=highest
    )


def per_device(
    hidden,
    x_weight,
    z_weight,
    bc_weight,
    dt_weight,
    conv_x,
    conv_bc,
    dt_bias,
    decay_rate,
    skip_gain,
    norm_gain,
    out_weight,
    lengths,
    owners,
):
    rows_here = hidden.shape[0]
    width_here = x_weight.shape[1]
    heads_here = dt_bias.shape[0]
    head_width = width_here // heads_here
    seq_count = lax.axis_size("seq")
    my_index = lax.axis_index("seq")
    first_row = my_index * rows_here
    prompt_end = jnp.cumsum(lengths)
    prompt_start = prompt_end - lengths
    positions = first_row + jnp.arange(rows_here, dtype=jnp.int32)
    segment = segment_of(positions, prompt_end)
    piece = lax.all_gather(hidden, "tp", axis=1, tiled=True)
    tp_count = lax.axis_size("tp")
    tp_index = lax.axis_index("tp")
    by_shift = [bc_weight] + [
        lax.ppermute(bc_weight, "tp", [(j, (j + s) % tp_count) for j in range(tp_count)])
        for s in range(1, tp_count)
    ]
    shift_of = (tp_index - jnp.arange(tp_count, dtype=jnp.int32)) % tp_count
    bc_full = jnp.concatenate(
        [jnp.take(jnp.stack(by_shift), shift_of[k], axis=0) for k in range(tp_count)], axis=1
    )

    def take(matrix):
        return jnp.dot(piece, matrix, preferred_element_type=jnp.float32)

    x_acc = take(x_weight)
    z_acc = take(z_weight)
    dt_raw = take(dt_weight)
    bc_acc = take(bc_full)
    x_in = x_acc.astype(jnp.bfloat16)
    z_in = z_acc.astype(jnp.bfloat16)
    bc_in = bc_acc.astype(jnp.bfloat16)
    joined = jnp.concatenate([x_in, bc_in], axis=1)
    earlier = passed_along(joined[rows_here - (KCONV - 1) :], "seq", 1)
    extended = jnp.concatenate([earlier, joined], axis=0)
    seg_ext = jnp.concatenate(
        [
            segment_of(
                first_row - (KCONV - 1) + jnp.arange(KCONV - 1, dtype=jnp.int32), prompt_end
            ),
            segment,
        ]
    )
    kernel = jnp.concatenate([conv_x, conv_bc], axis=1)
    mixed_in = short_conv(extended, seg_ext, kernel)
    x_conv = mixed_in[:, :width_here].astype(jnp.float32).reshape(rows_here, heads_here, head_width)
    b_conv = mixed_in[:, width_here : width_here + NS].astype(jnp.float32)
    c_conv = mixed_in[:, width_here + NS :].astype(jnp.float32)
    step_size = jax.nn.softplus(dt_raw + dt_bias[None, :])
    log_decay = -decay_rate[None, :] * step_size
    device_prior = segment_of(jnp.reshape(first_row - 1, (1,)), prompt_end)[0]
    level = jnp.cumsum(log_decay, axis=0)
    closing = segment[rows_here - 1]
    through = jnp.where(closing == device_prior, jnp.exp(level[rows_here - 1]), 0.0)
    tail = (
        jnp.where(
            (segment == closing)[:, None], jnp.exp(level[rows_here - 1][None, :] - level), 0.0
        )
        * step_size
    )
    local_end = jnp.einsum("jh,jhp,jn->hpn", tail, x_conv, b_conv, precision=highest)
    state_cols = head_width * NS
    packed_end = jnp.concatenate(
        [
            local_end.reshape(heads_here, state_cols),
            jnp.broadcast_to(through[:, None], (heads_here, 128)),
        ],
        axis=1,
    )
    gathered = lax.all_gather(packed_end, "seq")
    throughs = gathered[:, :, state_cols]
    source = jnp.arange(seq_count, dtype=jnp.int32)
    between = (source[None, :] > source[:, None]) & (source[None, :] < my_index)
    factors = jnp.where(between[:, :, None], throughs[None, :, :], 1.0)
    weights = jnp.where((source < my_index)[:, None], jnp.prod(factors, axis=1), 0.0)
    entering = jnp.sum(weights[:, :, None] * gathered[:, :, :state_cols], axis=0).reshape(
        heads_here, head_width, NS
    )

    blocks = rows_here // GROUP
    state = jnp.zeros((heads_here, head_width, NS), jnp.float32)
    pieces = []
    for blk in range(blocks):
        rows = slice(blk * GROUP, (blk + 1) * GROUP)
        seg_prior = device_prior if blk == 0 else segment[blk * GROUP - 1]
        state, output = advance_block(
            state,
            (
                x_conv[rows],
                b_conv[rows],
                c_conv[rows],
                step_size[rows],
                log_decay[rows],
                segment[rows],
                seg_prior,
            ),
        )
        pieces.append(output)
    ssm = jnp.concatenate(pieces, axis=0)
    inflow = jnp.where((segment == device_prior)[:, None], jnp.exp(level), 0.0)
    ssm = ssm + inflow[:, :, None] * jnp.einsum("in,hpn->ihp", c_conv, entering, precision=highest)
    ssm = ssm + skip_gain[None, :, None] * x_conv
    gated = ssm.reshape(rows_here, width_here) * jax.nn.silu(z_in.astype(jnp.float32))
    square_sum = lax.psum(jnp.sum(gated * gated, axis=1), "tp")
    normed = (gated * lax.rsqrt(square_sum / DIN + epsilon)[:, None] * norm_gain[None, :]).astype(
        jnp.bfloat16
    )
    mixed_cols = lax.psum_scatter(
        lax.dot_general(
            out_weight, normed, (((0,), (1,)), ((), ())), preferred_element_type=jnp.float32
        ).astype(jnp.bfloat16),
        "tp",
        scatter_dimension=0,
        tiled=True,
    )
    mixed = mixed_cols.T
    last_row = prompt_end - 1
    holder = last_row // rows_here
    present = holder == my_index
    inner = jnp.clip(last_row - first_row, 0, rows_here - 1)

    def finish(prompt_id, inner_row):
        return state_at(
            entering,
            device_prior,
            x_conv,
            b_conv,
            step_size,
            log_decay,
            segment,
            inner_row,
            prompt_id,
        )

    finals = jax.vmap(finish)(jnp.arange(PROMPTS, dtype=jnp.int32), inner)
    finals = jnp.where(present[:, None, None, None], finals, 0.0)

    def edge_of(inner_row, start_row, end_row):
        window = lax.dynamic_slice_in_dim(extended, inner_row + 1, KCONV - 1, 0)
        rows_global = end_row - (KCONV - 2) + jnp.arange(KCONV - 1, dtype=jnp.int32)
        return jnp.where((rows_global >= start_row)[:, None], window, jnp.zeros_like(window))

    edges = jax.vmap(edge_of)(inner, prompt_start, last_row)
    edges = jnp.where(present[:, None, None], edges.astype(jnp.float32), 0.0)
    edge_cols = (KCONV - 1) * edges.shape[2]
    combined = jnp.concatenate(
        [finals.reshape(PROMPTS, heads_here * state_cols), edges.reshape(PROMPTS, edge_cols)],
        axis=1,
    )
    combined_all = lax.psum(combined.astype(jnp.bfloat16), "seq").astype(jnp.float32)
    keeper = owners[0]
    kept = combined_all[keeper]
    final_state = kept[: heads_here * state_cols].reshape(1, heads_here, head_width, NS)
    kept_edges = kept[heads_here * state_cols :].reshape(KCONV - 1, edges.shape[2])
    conv_edge_x = kept_edges[:, :width_here].astype(jnp.bfloat16)[None]
    conv_edge_bc = kept_edges[:, width_here:].astype(jnp.bfloat16)[None]
    return (mixed, final_state, conv_edge_x, conv_edge_bc)


def solution(mesh):
    return jax.shard_map(
        per_device,
        mesh=mesh,
        in_specs=(
            P("seq", "tp"),
            P(None, "tp"),
            P(None, "tp"),
            P(None, "tp"),
            P(None, "tp"),
            P(None, "tp"),
            P(),
            P("tp"),
            P("tp"),
            P("tp"),
            P("tp"),
            P("tp", None),
            P(),
            P("seq"),
        ),
        out_specs=(
            P("seq", "tp"),
            P("seq", "tp", None, None),
            P("seq", None, "tp"),
            P("seq", None, None),
        ),
        check_vma=False,
    )
```

```python
import jax
import jax.numpy as jnp
from jax import lax
from jax.sharding import PartitionSpec as P

NS = 128
KCONV = 4
GROUP = 256
PROMPTS = 4
DIN = 4096


highest = lax.Precision.HIGHEST
epsilon = 1e-05


def passed_along(block, axis, distance):
    devices = range(lax.axis_size(axis))
    route = [(i - distance, i) for i in devices if i - distance in devices]
    return lax.ppermute(block, axis, route)


def segment_of(positions, prompt_end):
    counted = jnp.sum((positions[:, None] >= prompt_end[None, :]).astype(jnp.int32), axis=1)
    return jnp.where(positions < 0, -1, counted)


def short_conv(extended, seg_ext, kernel):
    taps = kernel.shape[0]
    count = extended.shape[0] - taps + 1
    total = jnp.zeros((count, extended.shape[1]), jnp.float32)
    for offset in range(taps):
        same = (seg_ext[offset : offset + count] == seg_ext[taps - 1 :]).astype(jnp.float32)
        total = (
            total
            + extended[offset : offset + count].astype(jnp.float32)
            * kernel[offset][None, :]
            * same[:, None]
        )
    return jax.nn.silu(total).astype(jnp.bfloat16)


def advance_block(state, block):
    x_blk, b_blk, c_blk, dt_blk, log_blk, seg_blk, seg_prior = block
    length = seg_blk.shape[0]
    acum = jnp.cumsum(log_blk, axis=0)
    index = jnp.arange(length, dtype=jnp.int32)
    keep = (seg_blk[:, None] == seg_blk[None, :]) & (index[:, None] >= index[None, :])
    spread = acum[:, None, :] - acum[None, :, :]
    decay = jnp.where(keep[:, :, None], jnp.exp(jnp.where(keep[:, :, None], spread, 0.0)), 0.0)
    scores = jnp.dot(c_blk, b_blk.T, precision=highest)
    mixing = scores[:, :, None] * decay * dt_blk[None, :, :]
    output = jnp.einsum("ijh,jhp->ihp", mixing, x_blk, precision=highest)
    inflow = jnp.where((seg_blk == seg_prior)[:, None], jnp.exp(acum), 0.0)
    output = output + inflow[:, :, None] * jnp.einsum(
        "in,hpn->ihp", c_blk, state, precision=highest
    )
    closing = seg_blk[length - 1]
    tail = (
        jnp.where((seg_blk == closing)[:, None], jnp.exp(acum[length - 1][None, :] - acum), 0.0)
        * dt_blk
    )
    fresh = jnp.einsum("jh,jhp,jn->hpn", tail, x_blk, b_blk, precision=highest)
    carry = jnp.where(closing == seg_prior, jnp.exp(acum[length - 1]), 0.0)
    return carry[:, None, None] * state + fresh, output


def state_at(start_state, seg_prior, x_rows, b_rows, dt_rows, log_rows, seg_rows, inner, prompt):
    acum = jnp.cumsum(log_rows, axis=0)
    level = acum[inner]
    index = jnp.arange(seg_rows.shape[0], dtype=jnp.int32)
    chosen = (seg_rows == prompt) & (index <= inner)
    weight = (
        jnp.where(
            chosen[:, None], jnp.exp(jnp.where(chosen[:, None], level[None, :] - acum, 0.0)), 0.0
        )
        * dt_rows
    )
    inflow = jnp.where(seg_rows[inner] == seg_prior, jnp.exp(level), 0.0)
    return inflow[:, None, None] * start_state + jnp.einsum(
        "jh,jhp,jn->hpn", weight, x_rows, b_rows, precision=highest
    )


def partial_at(seg_prior, x_rows, b_rows, dt_rows, level_rows, seg_rows, inner, prompt):
    level = level_rows[inner]
    index = jnp.arange(seg_rows.shape[0], dtype=jnp.int32)
    chosen = (seg_rows == prompt) & (index <= inner)
    weight = (
        jnp.where(
            chosen[:, None],
            jnp.exp(jnp.where(chosen[:, None], level[None, :] - level_rows, 0.0)),
            0.0,
        )
        * dt_rows
    )
    inflow = jnp.where(seg_rows[inner] == seg_prior, jnp.exp(level), 0.0)
    return jnp.einsum("jh,jhp,jn->hpn", weight, x_rows, b_rows, precision=highest), inflow


def tree_allreduce(big, small, axis, count):
    me = lax.axis_index(axis)
    order = [d for d in (1, 2, 8, 4, 16) if d < count]
    assert sorted(order) == [1 << k for k in range(count.bit_length() - 1)]
    for d in order:
        pairs = [(j, j ^ d) for j in range(count)]
        half = big.shape[0] // 2
        upper = (me // d) % 2
        send = lax.dynamic_slice_in_dim(big, (1 - upper) * half, half, 0)
        keep = lax.dynamic_slice_in_dim(big, upper * half, half, 0)
        got, got_small = lax.ppermute((send, small), axis, pairs)
        big = keep + got
        small = small + got_small
    for d in reversed(order):
        pairs = [(j, j ^ d) for j in range(count)]
        upper = (me // d) % 2 == 1
        got = lax.ppermute(big, axis, pairs)
        low = jnp.where(upper, got, big)
        high = jnp.where(upper, big, got)
        big = jnp.concatenate([low, high], axis=0)
    return big, small


def per_device(
    hidden,
    x_weight,
    z_weight,
    bc_weight,
    dt_weight,
    conv_x,
    conv_bc,
    dt_bias,
    decay_rate,
    skip_gain,
    norm_gain,
    out_weight,
    lengths,
    owners,
):
    rows_here = hidden.shape[0]
    width_here = x_weight.shape[1]
    heads_here = dt_bias.shape[0]
    head_width = width_here // heads_here
    seq_count = lax.axis_size("seq")
    my_index = lax.axis_index("seq")
    first_row = my_index * rows_here
    prompt_end = jnp.cumsum(lengths)
    prompt_start = prompt_end - lengths
    positions = first_row + jnp.arange(rows_here, dtype=jnp.int32)
    segment = segment_of(positions, prompt_end)
    piece = lax.all_gather(hidden, "tp", axis=1, tiled=True)
    tp_count = lax.axis_size("tp")
    tp_index = lax.axis_index("tp")
    by_shift = [bc_weight] + [
        lax.ppermute(bc_weight, "tp", [(j, (j + s) % tp_count) for j in range(tp_count)])
        for s in range(1, tp_count)
    ]
    shift_of = (tp_index - jnp.arange(tp_count, dtype=jnp.int32)) % tp_count
    bc_full = jnp.concatenate(
        [jnp.take(jnp.stack(by_shift), shift_of[k], axis=0) for k in range(tp_count)], axis=1
    )

    def take(matrix):
        return jnp.dot(piece, matrix, preferred_element_type=jnp.float32)

    x_acc = take(x_weight)
    z_acc = take(z_weight)
    dt_raw = take(dt_weight)
    bc_acc = take(bc_full)
    x_in = x_acc.astype(jnp.bfloat16)
    z_in = z_acc.astype(jnp.bfloat16)
    bc_in = bc_acc.astype(jnp.bfloat16)
    joined = jnp.concatenate([x_in, bc_in], axis=1)
    earlier = passed_along(joined[rows_here - (KCONV - 1) :], "seq", 1)
    extended = jnp.concatenate([earlier, joined], axis=0)
    seg_ext = jnp.concatenate(
        [
            segment_of(
                first_row - (KCONV - 1) + jnp.arange(KCONV - 1, dtype=jnp.int32), prompt_end
            ),
            segment,
        ]
    )
    kernel = jnp.concatenate([conv_x, conv_bc], axis=1)
    mixed_in = short_conv(extended, seg_ext, kernel)
    x_conv = mixed_in[:, :width_here].astype(jnp.float32).reshape(rows_here, heads_here, head_width)
    b_conv = mixed_in[:, width_here : width_here + NS].astype(jnp.float32)
    c_conv = mixed_in[:, width_here + NS :].astype(jnp.float32)
    step_size = jax.nn.softplus(dt_raw + dt_bias[None, :])
    log_decay = -decay_rate[None, :] * step_size
    device_prior = segment_of(jnp.reshape(first_row - 1, (1,)), prompt_end)[0]
    level = jnp.cumsum(log_decay, axis=0)
    closing = segment[rows_here - 1]
    through = jnp.where(closing == device_prior, jnp.exp(level[rows_here - 1]), 0.0)
    tail = (
        jnp.where(
            (segment == closing)[:, None], jnp.exp(level[rows_here - 1][None, :] - level), 0.0
        )
        * step_size
    )
    local_end = jnp.einsum("jh,jhp,jn->hpn", tail, x_conv, b_conv, precision=highest)
    state_cols = head_width * NS
    packed_end = jnp.concatenate(
        [
            local_end.reshape(heads_here, state_cols),
            jnp.broadcast_to(through[:, None], (heads_here, 128)),
        ],
        axis=1,
    )
    gathered = lax.all_gather(packed_end, "seq")
    throughs = gathered[:, :, state_cols]
    source = jnp.arange(seq_count, dtype=jnp.int32)
    between = (source[None, :] > source[:, None]) & (source[None, :] < my_index)
    factors = jnp.where(between[:, :, None], throughs[None, :, :], 1.0)
    weights = jnp.where((source < my_index)[:, None], jnp.prod(factors, axis=1), 0.0)
    entering = jnp.sum(weights[:, :, None] * gathered[:, :, :state_cols], axis=0).reshape(
        heads_here, head_width, NS
    )

    blocks = rows_here // GROUP
    state = jnp.zeros((heads_here, head_width, NS), jnp.float32)
    pieces = []
    for blk in range(blocks):
        rows = slice(blk * GROUP, (blk + 1) * GROUP)
        seg_prior = device_prior if blk == 0 else segment[blk * GROUP - 1]
        state, output = advance_block(
            state,
            (
                x_conv[rows],
                b_conv[rows],
                c_conv[rows],
                step_size[rows],
                log_decay[rows],
                segment[rows],
                seg_prior,
            ),
        )
        pieces.append(output)
    ssm = jnp.concatenate(pieces, axis=0)
    inflow = jnp.where((segment == device_prior)[:, None], jnp.exp(level), 0.0)
    ssm = ssm + inflow[:, :, None] * jnp.einsum("in,hpn->ihp", c_conv, entering, precision=highest)
    ssm = ssm + skip_gain[None, :, None] * x_conv
    gated = ssm.reshape(rows_here, width_here) * jax.nn.silu(z_in.astype(jnp.float32))
    square_sum = lax.psum(jnp.sum(gated * gated, axis=1), "tp")
    normed = (gated * lax.rsqrt(square_sum / DIN + epsilon)[:, None] * norm_gain[None, :]).astype(
        jnp.bfloat16
    )
    mixed_cols = lax.psum_scatter(
        lax.dot_general(
            out_weight, normed, (((0,), (1,)), ((), ())), preferred_element_type=jnp.float32
        ).astype(jnp.bfloat16),
        "tp",
        scatter_dimension=0,
        tiled=True,
    )
    mixed = mixed_cols.T
    last_row = prompt_end - 1
    holder = last_row // rows_here
    present = holder == my_index
    inner = jnp.clip(last_row - first_row, 0, rows_here - 1)

    def finish(prompt_id, inner_row):
        return partial_at(
            device_prior, x_conv, b_conv, step_size, level, segment, inner_row, prompt_id
        )

    partials, factors_at = jax.vmap(finish)(jnp.arange(PROMPTS, dtype=jnp.int32), inner)
    partials = jnp.where(present[:, None, None, None], partials, 0.0)
    factors_at = jnp.where(present[:, None], factors_at, 0.0)

    def edge_of(inner_row, start_row, end_row):
        window = lax.dynamic_slice_in_dim(extended, inner_row + 1, KCONV - 1, 0)
        rows_global = end_row - (KCONV - 2) + jnp.arange(KCONV - 1, dtype=jnp.int32)
        return jnp.where((rows_global >= start_row)[:, None], window, jnp.zeros_like(window))

    edges = jax.vmap(edge_of)(inner, prompt_start, last_row)
    edges = jnp.where(present[:, None, None], edges, jnp.zeros_like(edges))
    edge_cols = (KCONV - 1) * edges.shape[2]
    slot_rows = -(-(heads_here * state_cols + edge_cols) // 128)
    total_rows = PROMPTS * slot_rows
    padded_rows = -(-total_rows // (16 * seq_count)) * 16 * seq_count
    payload = jnp.concatenate(
        [
            partials.reshape(PROMPTS, heads_here * state_cols).astype(jnp.bfloat16),
            edges.reshape(PROMPTS, edge_cols),
            jnp.zeros((PROMPTS, slot_rows * 128 - heads_here * state_cols - edge_cols), jnp.bfloat16),
        ],
        axis=1,
    ).reshape(total_rows, 128)
    payload = jnp.concatenate(
        [payload, jnp.zeros((padded_rows - total_rows, 128), jnp.bfloat16)], axis=0
    )
    summed, factors_all = tree_allreduce(payload, factors_at, "seq", seq_count)
    keeper = owners[0]
    kept = summed[:total_rows].reshape(PROMPTS, slot_rows * 128)[keeper]
    target = holder[keeper]
    between_t = (source[None, :] > source[:, None]) & (source[None, :] < target)
    factors_t = jnp.where(between_t[:, :, None], throughs[None, :, :], 1.0)
    weights_t = jnp.where((source < target)[:, None], jnp.prod(factors_t, axis=1), 0.0)
    entering_t = jnp.sum(weights_t[:, :, None] * gathered[:, :, :state_cols], axis=0)
    final_flat = (
        factors_all[keeper][:, None] * entering_t
        + kept[: heads_here * state_cols].astype(jnp.float32).reshape(heads_here, state_cols)
    )
    final_state = final_flat.reshape(1, heads_here, head_width, NS)
    kept_edges = kept[heads_here * state_cols : heads_here * state_cols + edge_cols].reshape(
        KCONV - 1, edges.shape[2]
    )
    conv_edge_x = kept_edges[:, :width_here][None]
    conv_edge_bc = kept_edges[:, width_here:][None]
    return (mixed, final_state, conv_edge_x, conv_edge_bc)


def solution(mesh):
    return jax.shard_map(
        per_device,
        mesh=mesh,
        in_specs=(
            P("seq", "tp"),
            P(None, "tp"),
            P(None, "tp"),
            P(None, "tp"),
            P(None, "tp"),
            P(None, "tp"),
            P(),
            P("tp"),
            P("tp"),
            P("tp"),
            P("tp"),
            P("tp", None),
            P(),
            P("seq"),
        ),
        out_specs=(
            P("seq", "tp"),
            P("seq", "tp", None, None),
            P("seq", None, "tp"),
            P("seq", None, None),
        ),
        check_vma=False,
    )
```

```python
import jax
import jax.numpy as jnp
from jax import lax
from jax.sharding import PartitionSpec as P

NS = 128
KCONV = 4
GROUP = 256
PROMPTS = 4
DIN = 4096


highest = lax.Precision.HIGHEST
high = lax.Precision.HIGH
epsilon = 1e-05


def passed_along(block, axis, distance):
    devices = range(lax.axis_size(axis))
    route = [(i - distance, i) for i in devices if i - distance in devices]
    return lax.ppermute(block, axis, route)


def segment_of(positions, prompt_end):
    counted = jnp.sum((positions[:, None] >= prompt_end[None, :]).astype(jnp.int32), axis=1)
    return jnp.where(positions < 0, -1, counted)


def short_conv(extended, seg_ext, kernel):
    taps = kernel.shape[0]
    count = extended.shape[0] - taps + 1
    total = jnp.zeros((count, extended.shape[1]), jnp.float32)
    for offset in range(taps):
        same = (seg_ext[offset : offset + count] == seg_ext[taps - 1 :]).astype(jnp.float32)
        total = (
            total
            + extended[offset : offset + count].astype(jnp.float32)
            * kernel[offset][None, :]
            * same[:, None]
        )
    return jax.nn.silu(total).astype(jnp.bfloat16)


def advance_block(state, block):
    x_blk, b_blk, c_blk, dt_blk, log_blk, seg_blk, seg_prior = block
    length = seg_blk.shape[0]
    acum = jnp.cumsum(log_blk, axis=0)
    index = jnp.arange(length, dtype=jnp.int32)
    keep = (seg_blk[:, None] == seg_blk[None, :]) & (index[:, None] >= index[None, :])
    spread = acum[:, None, :] - acum[None, :, :]
    decay = jnp.where(keep[:, :, None], jnp.exp(jnp.where(keep[:, :, None], spread, 0.0)), 0.0)
    scores = jnp.dot(c_blk.astype(jnp.bfloat16), b_blk.T.astype(jnp.bfloat16), preferred_element_type=jnp.float32)
    mixing = scores[:, :, None] * decay * dt_blk[None, :, :]
    output = jnp.einsum("ijh,jhp->ihp", mixing, x_blk, precision=high)
    inflow = jnp.where((seg_blk == seg_prior)[:, None], jnp.exp(acum), 0.0)
    output = output + inflow[:, :, None] * jnp.einsum(
        "in,hpn->ihp", c_blk, state, precision=high
    )
    closing = seg_blk[length - 1]
    tail = (
        jnp.where((seg_blk == closing)[:, None], jnp.exp(acum[length - 1][None, :] - acum), 0.0)
        * dt_blk
    )
    fresh = jnp.einsum("jh,jhp,jn->hpn", tail, x_blk, b_blk, precision=high)
    carry = jnp.where(closing == seg_prior, jnp.exp(acum[length - 1]), 0.0)
    return carry[:, None, None] * state + fresh, output


def state_at(start_state, seg_prior, x_rows, b_rows, dt_rows, log_rows, seg_rows, inner, prompt):
    acum = jnp.cumsum(log_rows, axis=0)
    level = acum[inner]
    index = jnp.arange(seg_rows.shape[0], dtype=jnp.int32)
    chosen = (seg_rows == prompt) & (index <= inner)
    weight = (
        jnp.where(
            chosen[:, None], jnp.exp(jnp.where(chosen[:, None], level[None, :] - acum, 0.0)), 0.0
        )
        * dt_rows
    )
    inflow = jnp.where(seg_rows[inner] == seg_prior, jnp.exp(level), 0.0)
    return inflow[:, None, None] * start_state + jnp.einsum(
        "jh,jhp,jn->hpn", weight, x_rows, b_rows, precision=highest
    )


def partial_at(seg_prior, x_rows, b_rows, dt_rows, level_rows, seg_rows, inner, prompt):
    level = level_rows[inner]
    index = jnp.arange(seg_rows.shape[0], dtype=jnp.int32)
    chosen = (seg_rows == prompt) & (index <= inner)
    weight = (
        jnp.where(
            chosen[:, None],
            jnp.exp(jnp.where(chosen[:, None], level[None, :] - level_rows, 0.0)),
            0.0,
        )
        * dt_rows
    )
    inflow = jnp.where(seg_rows[inner] == seg_prior, jnp.exp(level), 0.0)
    return jnp.einsum("jh,jhp,jn->hpn", weight, x_rows, b_rows, precision=high), inflow


def tree_allreduce(big, small, axis, count):
    me = lax.axis_index(axis)
    order = [d for d in (1, 2, 8, 4, 16) if d < count]
    assert sorted(order) == [1 << k for k in range(count.bit_length() - 1)]
    for d in order:
        pairs = [(j, j ^ d) for j in range(count)]
        half = big.shape[0] // 2
        upper = (me // d) % 2
        send = lax.dynamic_slice_in_dim(big, (1 - upper) * half, half, 0)
        keep = lax.dynamic_slice_in_dim(big, upper * half, half, 0)
        got, got_small = lax.ppermute((send, small), axis, pairs)
        big = keep + got
        small = small + got_small
    for d in reversed(order):
        pairs = [(j, j ^ d) for j in range(count)]
        upper = (me // d) % 2 == 1
        got = lax.ppermute(big, axis, pairs)
        low = jnp.where(upper, got, big)
        high = jnp.where(upper, big, got)
        big = jnp.concatenate([low, high], axis=0)
    return big, small


def per_device(
    hidden,
    x_weight,
    z_weight,
    bc_weight,
    dt_weight,
    conv_x,
    conv_bc,
    dt_bias,
    decay_rate,
    skip_gain,
    norm_gain,
    out_weight,
    lengths,
    owners,
):
    rows_here = hidden.shape[0]
    width_here = x_weight.shape[1]
    heads_here = dt_bias.shape[0]
    head_width = width_here // heads_here
    seq_count = lax.axis_size("seq")
    my_index = lax.axis_index("seq")
    first_row = my_index * rows_here
    prompt_end = jnp.cumsum(lengths)
    prompt_start = prompt_end - lengths
    positions = first_row + jnp.arange(rows_here, dtype=jnp.int32)
    segment = segment_of(positions, prompt_end)
    piece = lax.all_gather(hidden, "tp", axis=1, tiled=True)
    tp_count = lax.axis_size("tp")
    tp_index = lax.axis_index("tp")
    by_shift = [bc_weight] + [
        lax.ppermute(bc_weight, "tp", [(j, (j + s) % tp_count) for j in range(tp_count)])
        for s in range(1, tp_count)
    ]
    shift_of = (tp_index - jnp.arange(tp_count, dtype=jnp.int32)) % tp_count
    bc_full = jnp.concatenate(
        [jnp.take(jnp.stack(by_shift), shift_of[k], axis=0) for k in range(tp_count)], axis=1
    )

    def take(matrix):
        return jnp.dot(piece, matrix, preferred_element_type=jnp.float32)

    x_acc = take(x_weight)
    z_acc = take(z_weight)
    dt_raw = take(dt_weight)
    bc_acc = take(bc_full)
    x_in = x_acc.astype(jnp.bfloat16)
    z_in = z_acc.astype(jnp.bfloat16)
    bc_in = bc_acc.astype(jnp.bfloat16)
    joined = jnp.concatenate([x_in, bc_in], axis=1)
    earlier = passed_along(joined[rows_here - (KCONV - 1) :], "seq", 1)
    extended = jnp.concatenate([earlier, joined], axis=0)
    seg_ext = jnp.concatenate(
        [
            segment_of(
                first_row - (KCONV - 1) + jnp.arange(KCONV - 1, dtype=jnp.int32), prompt_end
            ),
            segment,
        ]
    )
    kernel = jnp.concatenate([conv_x, conv_bc], axis=1)
    mixed_in = short_conv(extended, seg_ext, kernel)
    x_conv = mixed_in[:, :width_here].astype(jnp.float32).reshape(rows_here, heads_here, head_width)
    b_conv = mixed_in[:, width_here : width_here + NS].astype(jnp.float32)
    c_conv = mixed_in[:, width_here + NS :].astype(jnp.float32)
    step_size = jax.nn.softplus(dt_raw + dt_bias[None, :])
    log_decay = -decay_rate[None, :] * step_size
    device_prior = segment_of(jnp.reshape(first_row - 1, (1,)), prompt_end)[0]
    level = jnp.cumsum(log_decay, axis=0)
    closing = segment[rows_here - 1]
    through = jnp.where(closing == device_prior, jnp.exp(level[rows_here - 1]), 0.0)
    tail = (
        jnp.where(
            (segment == closing)[:, None], jnp.exp(level[rows_here - 1][None, :] - level), 0.0
        )
        * step_size
    )
    local_end = jnp.einsum("jh,jhp,jn->hpn", tail, x_conv, b_conv, precision=high)
    state_cols = head_width * NS
    packed_end = jnp.concatenate(
        [
            local_end.reshape(heads_here, state_cols),
            jnp.broadcast_to(through[:, None], (heads_here, 128)),
        ],
        axis=1,
    )
    gathered = lax.all_gather(packed_end, "seq")
    throughs = gathered[:, :, state_cols]
    source = jnp.arange(seq_count, dtype=jnp.int32)
    last_row = prompt_end - 1
    holder = last_row // rows_here
    keeper = owners[0]
    targets = jnp.stack([my_index, holder[keeper]])
    between = (source[None, None, :] > source[None, :, None]) & (
        source[None, None, :] < targets[:, None, None]
    )
    factors = jnp.where(between[:, :, :, None], throughs[None, None, :, :], 1.0)
    weights = jnp.where(
        (source[None, :] < targets[:, None])[:, :, None], jnp.prod(factors, axis=2), 0.0
    )
    entering_both = jnp.einsum(
        "tjh,jhx->thx", weights, gathered[:, :, :state_cols], precision=highest
    )
    entering = entering_both[0].reshape(heads_here, head_width, NS)
    entering_t = entering_both[1]

    blocks = rows_here // GROUP
    state = jnp.zeros((heads_here, head_width, NS), jnp.float32)
    pieces = []
    for blk in range(blocks):
        rows = slice(blk * GROUP, (blk + 1) * GROUP)
        seg_prior = device_prior if blk == 0 else segment[blk * GROUP - 1]
        state, output = advance_block(
            state,
            (
                x_conv[rows],
                b_conv[rows],
                c_conv[rows],
                step_size[rows],
                log_decay[rows],
                segment[rows],
                seg_prior,
            ),
        )
        pieces.append(output)
    ssm = jnp.concatenate(pieces, axis=0)
    inflow = jnp.where((segment == device_prior)[:, None], jnp.exp(level), 0.0)
    ssm = ssm + inflow[:, :, None] * jnp.einsum("in,hpn->ihp", c_conv, entering, precision=high)
    ssm = ssm + skip_gain[None, :, None] * x_conv
    gated_all = ssm.reshape(rows_here, width_here) * jax.nn.silu(z_in.astype(jnp.float32))
    halves = []
    half_rows = rows_here // 2
    for part in range(2):
        gated = gated_all[part * half_rows : (part + 1) * half_rows]
        square_sum = lax.psum(jnp.sum(gated * gated, axis=1), "tp")
        normed = (
            gated * lax.rsqrt(square_sum / DIN + epsilon)[:, None] * norm_gain[None, :]
        ).astype(jnp.bfloat16)
        mixed_cols = lax.psum_scatter(
            lax.dot_general(
                out_weight, normed, (((0,), (1,)), ((), ())), preferred_element_type=jnp.float32
            ).astype(jnp.bfloat16),
            "tp",
            scatter_dimension=0,
            tiled=True,
        )
        halves.append(mixed_cols.T)
    mixed = jnp.concatenate(halves, axis=0)
    present = holder == my_index
    inner = jnp.clip(last_row - first_row, 0, rows_here - 1)

    def finish(prompt_id, inner_row):
        return partial_at(
            device_prior, x_conv, b_conv, step_size, level, segment, inner_row, prompt_id
        )

    partials, factors_at = jax.vmap(finish)(jnp.arange(PROMPTS, dtype=jnp.int32), inner)
    partials = jnp.where(present[:, None, None, None], partials, 0.0)
    factors_at = jnp.where(present[:, None], factors_at, 0.0)

    def edge_of(inner_row, start_row, end_row):
        window = lax.dynamic_slice_in_dim(extended, inner_row + 1, KCONV - 1, 0)
        rows_global = end_row - (KCONV - 2) + jnp.arange(KCONV - 1, dtype=jnp.int32)
        return jnp.where((rows_global >= start_row)[:, None], window, jnp.zeros_like(window))

    edges = jax.vmap(edge_of)(inner, prompt_start, last_row)
    edges = jnp.where(present[:, None, None], edges, jnp.zeros_like(edges))
    edge_cols = (KCONV - 1) * edges.shape[2]
    slot_rows = -(-(heads_here * state_cols + edge_cols) // 128)
    total_rows = PROMPTS * slot_rows
    padded_rows = -(-total_rows // (16 * seq_count)) * 16 * seq_count
    payload = jnp.concatenate(
        [
            partials.reshape(PROMPTS, heads_here * state_cols).astype(jnp.bfloat16),
            edges.reshape(PROMPTS, edge_cols),
            jnp.zeros((PROMPTS, slot_rows * 128 - heads_here * state_cols - edge_cols), jnp.bfloat16),
        ],
        axis=1,
    ).reshape(total_rows, 128)
    payload = jnp.concatenate(
        [payload, jnp.zeros((padded_rows - total_rows, 128), jnp.bfloat16)], axis=0
    )
    summed, factors_all = tree_allreduce(payload, factors_at, "seq", seq_count)
    kept = summed[:total_rows].reshape(PROMPTS, slot_rows * 128)[keeper]
    final_flat = (
        factors_all[keeper][:, None] * entering_t
        + kept[: heads_here * state_cols].astype(jnp.float32).reshape(heads_here, state_cols)
    )
    final_state = final_flat.reshape(1, heads_here, head_width, NS)
    kept_edges = kept[heads_here * state_cols : heads_here * state_cols + edge_cols].reshape(
        KCONV - 1, edges.shape[2]
    )
    conv_edge_x = kept_edges[:, :width_here][None]
    conv_edge_bc = kept_edges[:, width_here:][None]
    return (mixed, final_state, conv_edge_x, conv_edge_bc)


def solution(mesh):
    return jax.shard_map(
        per_device,
        mesh=mesh,
        in_specs=(
            P("seq", "tp"),
            P(None, "tp"),
            P(None, "tp"),
            P(None, "tp"),
            P(None, "tp"),
            P(None, "tp"),
            P(),
            P("tp"),
            P("tp"),
            P("tp"),
            P("tp"),
            P("tp", None),
            P(),
            P("seq"),
        ),
        out_specs=(
            P("seq", "tp"),
            P("seq", "tp", None, None),
            P("seq", None, "tp"),
            P("seq", None, None),
        ),
        check_vma=False,
    )
```

```python
import jax
import jax.numpy as jnp
from jax import lax
from jax.sharding import PartitionSpec as P

NS = 128
KCONV = 4
GROUP = 256
PROMPTS = 4
DIN = 4096


highest = lax.Precision.HIGHEST
high = lax.Precision.HIGH
epsilon = 1e-05


def passed_along(block, axis, distance):
    devices = range(lax.axis_size(axis))
    route = [(i - distance, i) for i in devices if i - distance in devices]
    return lax.ppermute(block, axis, route)


def segment_of(positions, prompt_end):
    counted = jnp.sum((positions[:, None] >= prompt_end[None, :]).astype(jnp.int32), axis=1)
    return jnp.where(positions < 0, -1, counted)


def short_conv(extended, seg_ext, kernel):
    taps = kernel.shape[0]
    count = extended.shape[0] - taps + 1
    total = jnp.zeros((count, extended.shape[1]), jnp.float32)
    for offset in range(taps):
        same = (seg_ext[offset : offset + count] == seg_ext[taps - 1 :]).astype(jnp.float32)
        total = (
            total
            + extended[offset : offset + count].astype(jnp.float32)
            * kernel[offset][None, :]
            * same[:, None]
        )
    return jax.nn.silu(total).astype(jnp.bfloat16)


def advance_block(state, block):
    x_blk, b_blk, c_blk, dt_blk, log_blk, seg_blk, seg_prior = block
    length = seg_blk.shape[0]
    acum = jnp.cumsum(log_blk, axis=0)
    index = jnp.arange(length, dtype=jnp.int32)
    keep = (seg_blk[:, None] == seg_blk[None, :]) & (index[:, None] >= index[None, :])
    spread = acum[:, None, :] - acum[None, :, :]
    decay = jnp.where(keep[:, :, None], jnp.exp(jnp.where(keep[:, :, None], spread, 0.0)), 0.0)
    scores = jnp.dot(c_blk.astype(jnp.bfloat16), b_blk.T.astype(jnp.bfloat16), preferred_element_type=jnp.float32)
    mixing = scores[:, :, None] * decay * dt_blk[None, :, :]
    output = jnp.einsum("ijh,jhp->ihp", mixing, x_blk, precision=high)
    inflow = jnp.where((seg_blk == seg_prior)[:, None], jnp.exp(acum), 0.0)
    output = output + inflow[:, :, None] * jnp.einsum(
        "in,hpn->ihp", c_blk, state, precision=high
    )
    closing = seg_blk[length - 1]
    tail = (
        jnp.where((seg_blk == closing)[:, None], jnp.exp(acum[length - 1][None, :] - acum), 0.0)
        * dt_blk
    )
    fresh = jnp.einsum("jh,jhp,jn->hpn", tail, x_blk, b_blk, precision=high)
    carry = jnp.where(closing == seg_prior, jnp.exp(acum[length - 1]), 0.0)
    return carry[:, None, None] * state + fresh, output


def state_at(start_state, seg_prior, x_rows, b_rows, dt_rows, log_rows, seg_rows, inner, prompt):
    acum = jnp.cumsum(log_rows, axis=0)
    level = acum[inner]
    index = jnp.arange(seg_rows.shape[0], dtype=jnp.int32)
    chosen = (seg_rows == prompt) & (index <= inner)
    weight = (
        jnp.where(
            chosen[:, None], jnp.exp(jnp.where(chosen[:, None], level[None, :] - acum, 0.0)), 0.0
        )
        * dt_rows
    )
    inflow = jnp.where(seg_rows[inner] == seg_prior, jnp.exp(level), 0.0)
    return inflow[:, None, None] * start_state + jnp.einsum(
        "jh,jhp,jn->hpn", weight, x_rows, b_rows, precision=highest
    )


def partial_at(seg_prior, x_rows, b_rows, dt_rows, level_rows, seg_rows, inner, prompt):
    level = level_rows[inner]
    index = jnp.arange(seg_rows.shape[0], dtype=jnp.int32)
    chosen = (seg_rows == prompt) & (index <= inner)
    weight = (
        jnp.where(
            chosen[:, None],
            jnp.exp(jnp.where(chosen[:, None], level[None, :] - level_rows, 0.0)),
            0.0,
        )
        * dt_rows
    )
    inflow = jnp.where(seg_rows[inner] == seg_prior, jnp.exp(level), 0.0)
    return jnp.einsum("jh,jhp,jn->hpn", weight, x_rows, b_rows, precision=high), inflow


def tree_allreduce(big, small, axis, count):
    me = lax.axis_index(axis)
    order = [d for d in (1, 2, 8, 4, 16) if d < count]
    assert sorted(order) == [1 << k for k in range(count.bit_length() - 1)]
    for d in order:
        pairs = [(j, j ^ d) for j in range(count)]
        half = big.shape[0] // 2
        upper = (me // d) % 2
        send = lax.dynamic_slice_in_dim(big, (1 - upper) * half, half, 0)
        keep = lax.dynamic_slice_in_dim(big, upper * half, half, 0)
        got, got_small = lax.ppermute((send, small), axis, pairs)
        big = keep + got
        small = small + got_small
    for d in reversed(order):
        pairs = [(j, j ^ d) for j in range(count)]
        upper = (me // d) % 2 == 1
        got = lax.ppermute(big, axis, pairs)
        low = jnp.where(upper, got, big)
        high = jnp.where(upper, big, got)
        big = jnp.concatenate([low, high], axis=0)
    return big, small


def per_device(
    hidden,
    x_weight,
    z_weight,
    bc_weight,
    dt_weight,
    conv_x,
    conv_bc,
    dt_bias,
    decay_rate,
    skip_gain,
    norm_gain,
    out_weight,
    lengths,
    owners,
):
    rows_here = hidden.shape[0]
    width_here = x_weight.shape[1]
    heads_here = dt_bias.shape[0]
    head_width = width_here // heads_here
    seq_count = lax.axis_size("seq")
    my_index = lax.axis_index("seq")
    first_row = my_index * rows_here
    prompt_end = jnp.cumsum(lengths)
    prompt_start = prompt_end - lengths
    positions = first_row + jnp.arange(rows_here, dtype=jnp.int32)
    segment = segment_of(positions, prompt_end)
    piece = lax.all_gather(hidden, "tp", axis=1, tiled=True)
    tp_count = lax.axis_size("tp")
    tp_index = lax.axis_index("tp")
    by_shift = [bc_weight] + [
        lax.ppermute(bc_weight, "tp", [(j, (j + s) % tp_count) for j in range(tp_count)])
        for s in range(1, tp_count)
    ]
    shift_of = (tp_index - jnp.arange(tp_count, dtype=jnp.int32)) % tp_count
    bc_full = jnp.concatenate(
        [jnp.take(jnp.stack(by_shift), shift_of[k], axis=0) for k in range(tp_count)], axis=1
    )

    def take(matrix):
        return jnp.dot(piece, matrix, preferred_element_type=jnp.float32)

    x_acc = take(x_weight)
    z_acc = take(z_weight)
    dt_raw = take(dt_weight)
    bc_acc = take(bc_full)
    x_in = x_acc.astype(jnp.bfloat16)
    z_in = z_acc.astype(jnp.bfloat16)
    bc_in = bc_acc.astype(jnp.bfloat16)
    joined = jnp.concatenate([x_in, bc_in], axis=1)
    earlier = passed_along(joined[rows_here - (KCONV - 1) :], "seq", 1)
    extended = jnp.concatenate([earlier, joined], axis=0)
    seg_ext = jnp.concatenate(
        [
            segment_of(
                first_row - (KCONV - 1) + jnp.arange(KCONV - 1, dtype=jnp.int32), prompt_end
            ),
            segment,
        ]
    )
    kernel = jnp.concatenate([conv_x, conv_bc], axis=1)
    mixed_in = short_conv(extended, seg_ext, kernel)
    x_conv = mixed_in[:, :width_here].astype(jnp.float32).reshape(rows_here, heads_here, head_width)
    b_conv = mixed_in[:, width_here : width_here + NS].astype(jnp.float32)
    c_conv = mixed_in[:, width_here + NS :].astype(jnp.float32)
    step_size = jax.nn.softplus(dt_raw + dt_bias[None, :])
    log_decay = -decay_rate[None, :] * step_size
    device_prior = segment_of(jnp.reshape(first_row - 1, (1,)), prompt_end)[0]
    level = jnp.cumsum(log_decay, axis=0)
    closing = segment[rows_here - 1]
    through = jnp.where(closing == device_prior, jnp.exp(level[rows_here - 1]), 0.0)
    tail = (
        jnp.where(
            (segment == closing)[:, None], jnp.exp(level[rows_here - 1][None, :] - level), 0.0
        )
        * step_size
    )
    local_end = jnp.einsum("jh,jhp,jn->hpn", tail, x_conv, b_conv, precision=high)
    state_cols = head_width * NS
    packed_end = jnp.concatenate(
        [
            local_end.reshape(heads_here, state_cols),
            jnp.broadcast_to(through[:, None], (heads_here, 128)),
        ],
        axis=1,
    )
    gathered = lax.all_gather(packed_end, "seq")
    throughs = gathered[:, :, state_cols]
    source = jnp.arange(seq_count, dtype=jnp.int32)
    last_row = prompt_end - 1
    holder = last_row // rows_here
    keeper = owners[0]

    def entering_of(target):
        between = (source[None, :] > source[:, None]) & (source[None, :] < target)
        factors = jnp.where(between[:, :, None], throughs[None, :, :], 1.0)
        weights = jnp.where((source < target)[:, None], jnp.prod(factors, axis=1), 0.0)
        return jnp.sum(weights[:, :, None] * gathered[:, :, :state_cols], axis=0)

    entering = entering_of(my_index).reshape(heads_here, head_width, NS)
    entering_t = entering_of(holder[keeper])

    blocks = rows_here // GROUP
    state = jnp.zeros((heads_here, head_width, NS), jnp.float32)
    pieces = []
    for blk in range(blocks):
        rows = slice(blk * GROUP, (blk + 1) * GROUP)
        seg_prior = device_prior if blk == 0 else segment[blk * GROUP - 1]
        state, output = advance_block(
            state,
            (
                x_conv[rows],
                b_conv[rows],
                c_conv[rows],
                step_size[rows],
                log_decay[rows],
                segment[rows],
                seg_prior,
            ),
        )
        pieces.append(output)
    ssm = jnp.concatenate(pieces, axis=0)
    inflow = jnp.where((segment == device_prior)[:, None], jnp.exp(level), 0.0)
    ssm = ssm + inflow[:, :, None] * jnp.einsum("in,hpn->ihp", c_conv, entering, precision=high)
    ssm = ssm + skip_gain[None, :, None] * x_conv
    gated_all = ssm.reshape(rows_here, width_here) * jax.nn.silu(z_in.astype(jnp.float32))
    halves = []
    half_rows = rows_here // 2
    for part in range(2):
        gated = gated_all[part * half_rows : (part + 1) * half_rows]
        square_sum = lax.psum(jnp.sum(gated * gated, axis=1), "tp")
        normed = (
            gated * lax.rsqrt(square_sum / DIN + epsilon)[:, None] * norm_gain[None, :]
        ).astype(jnp.bfloat16)
        mixed_cols = lax.psum_scatter(
            lax.dot_general(
                out_weight, normed, (((0,), (1,)), ((), ())), preferred_element_type=jnp.float32
            ).astype(jnp.bfloat16),
            "tp",
            scatter_dimension=0,
            tiled=True,
        )
        halves.append(mixed_cols.T)
    mixed = jnp.concatenate(halves, axis=0)
    present = holder == my_index
    inner = jnp.clip(last_row - first_row, 0, rows_here - 1)

    def finish(prompt_id, inner_row):
        return partial_at(
            device_prior, x_conv, b_conv, step_size, level, segment, inner_row, prompt_id
        )

    partials, factors_at = jax.vmap(finish)(jnp.arange(PROMPTS, dtype=jnp.int32), inner)
    partials = jnp.where(present[:, None, None, None], partials, 0.0)
    factors_at = jnp.where(present[:, None], factors_at, 0.0)

    def edge_of(inner_row, start_row, end_row):
        window = lax.dynamic_slice_in_dim(extended, inner_row + 1, KCONV - 1, 0)
        rows_global = end_row - (KCONV - 2) + jnp.arange(KCONV - 1, dtype=jnp.int32)
        return jnp.where((rows_global >= start_row)[:, None], window, jnp.zeros_like(window))

    edges = jnp.stack(
        [edge_of(inner[r], prompt_start[r], last_row[r]) for r in range(PROMPTS)]
    )
    edges = jnp.where(present[:, None, None], edges, jnp.zeros_like(edges))
    edge_cols = (KCONV - 1) * edges.shape[2]
    slot_rows = -(-(heads_here * state_cols + edge_cols) // 128)
    total_rows = PROMPTS * slot_rows
    padded_rows = -(-total_rows // (16 * seq_count)) * 16 * seq_count
    payload = jnp.concatenate(
        [
            partials.reshape(PROMPTS, heads_here * state_cols).astype(jnp.bfloat16),
            edges.reshape(PROMPTS, edge_cols),
            jnp.zeros((PROMPTS, slot_rows * 128 - heads_here * state_cols - edge_cols), jnp.bfloat16),
        ],
        axis=1,
    ).reshape(total_rows, 128)
    payload = jnp.concatenate(
        [payload, jnp.zeros((padded_rows - total_rows, 128), jnp.bfloat16)], axis=0
    )
    summed, factors_all = tree_allreduce(payload, factors_at, "seq", seq_count)
    kept = summed[:total_rows].reshape(PROMPTS, slot_rows * 128)[keeper]
    final_flat = (
        factors_all[keeper][:, None] * entering_t
        + kept[: heads_here * state_cols].astype(jnp.float32).reshape(heads_here, state_cols)
    )
    final_state = final_flat.reshape(1, heads_here, head_width, NS)
    kept_edges = kept[heads_here * state_cols : heads_here * state_cols + edge_cols].reshape(
        KCONV - 1, edges.shape[2]
    )
    conv_edge_x = kept_edges[:, :width_here][None]
    conv_edge_bc = kept_edges[:, width_here:][None]
    return (mixed, final_state, conv_edge_x, conv_edge_bc)


def solution(mesh):
    return jax.shard_map(
        per_device,
        mesh=mesh,
        in_specs=(
            P("seq", "tp"),
            P(None, "tp"),
            P(None, "tp"),
            P(None, "tp"),
            P(None, "tp"),
            P(None, "tp"),
            P(),
            P("tp"),
            P("tp"),
            P("tp"),
            P("tp"),
            P("tp", None),
            P(),
            P("seq"),
        ),
        out_specs=(
            P("seq", "tp"),
            P("seq", "tp", None, None),
            P("seq", None, "tp"),
            P("seq", None, None),
        ),
        check_vma=False,
    )
```

```python
import jax
import jax.numpy as jnp
from jax import lax
from jax.sharding import PartitionSpec as P

NS = 128
KCONV = 4
GROUP = 256
PROMPTS = 4
DIN = 4096


highest = lax.Precision.HIGHEST
high = lax.Precision.HIGH
epsilon = 1e-05


def passed_along(block, axis, distance):
    devices = range(lax.axis_size(axis))
    route = [(i - distance, i) for i in devices if i - distance in devices]
    return lax.ppermute(block, axis, route)


def segment_of(positions, prompt_end):
    counted = jnp.sum((positions[:, None] >= prompt_end[None, :]).astype(jnp.int32), axis=1)
    return jnp.where(positions < 0, -1, counted)


def short_conv(extended, seg_ext, kernel):
    taps = kernel.shape[0]
    count = extended.shape[0] - taps + 1
    total = jnp.zeros((count, extended.shape[1]), jnp.float32)
    for offset in range(taps):
        same = (seg_ext[offset : offset + count] == seg_ext[taps - 1 :]).astype(jnp.float32)
        total = (
            total
            + extended[offset : offset + count].astype(jnp.float32)
            * kernel[offset][None, :]
            * same[:, None]
        )
    return jax.nn.silu(total).astype(jnp.bfloat16)


def advance_block(state, block):
    x_blk, b_blk, c_blk, dt_blk, log_blk, seg_blk, seg_prior = block
    length = seg_blk.shape[0]
    acum = jnp.cumsum(log_blk, axis=0)
    index = jnp.arange(length, dtype=jnp.int32)
    keep = (seg_blk[:, None] == seg_blk[None, :]) & (index[:, None] >= index[None, :])
    spread = acum[:, None, :] - acum[None, :, :]
    decay = jnp.where(keep[:, :, None], jnp.exp(jnp.where(keep[:, :, None], spread, 0.0)), 0.0)
    scores = jnp.dot(c_blk.astype(jnp.bfloat16), b_blk.T.astype(jnp.bfloat16), preferred_element_type=jnp.float32)
    mixing = scores[:, :, None] * decay * dt_blk[None, :, :]
    output = jnp.einsum("ijh,jhp->ihp", mixing, x_blk, precision=high)
    inflow = jnp.where((seg_blk == seg_prior)[:, None], jnp.exp(acum), 0.0)
    output = output + inflow[:, :, None] * jnp.einsum(
        "in,hpn->ihp", c_blk, state, precision=high
    )
    closing = seg_blk[length - 1]
    tail = (
        jnp.where((seg_blk == closing)[:, None], jnp.exp(acum[length - 1][None, :] - acum), 0.0)
        * dt_blk
    )
    fresh = jnp.einsum("jh,jhp,jn->hpn", tail, x_blk, b_blk, precision=high)
    carry = jnp.where(closing == seg_prior, jnp.exp(acum[length - 1]), 0.0)
    return carry[:, None, None] * state + fresh, output


def state_at(start_state, seg_prior, x_rows, b_rows, dt_rows, log_rows, seg_rows, inner, prompt):
    acum = jnp.cumsum(log_rows, axis=0)
    level = acum[inner]
    index = jnp.arange(seg_rows.shape[0], dtype=jnp.int32)
    chosen = (seg_rows == prompt) & (index <= inner)
    weight = (
        jnp.where(
            chosen[:, None], jnp.exp(jnp.where(chosen[:, None], level[None, :] - acum, 0.0)), 0.0
        )
        * dt_rows
    )
    inflow = jnp.where(seg_rows[inner] == seg_prior, jnp.exp(level), 0.0)
    return inflow[:, None, None] * start_state + jnp.einsum(
        "jh,jhp,jn->hpn", weight, x_rows, b_rows, precision=highest
    )


def partial_at(seg_prior, x_rows, b_rows, dt_rows, level_rows, seg_rows, inner, prompt):
    level = level_rows[inner]
    index = jnp.arange(seg_rows.shape[0], dtype=jnp.int32)
    chosen = (seg_rows == prompt) & (index <= inner)
    weight = (
        jnp.where(
            chosen[:, None],
            jnp.exp(jnp.where(chosen[:, None], level[None, :] - level_rows, 0.0)),
            0.0,
        )
        * dt_rows
    )
    inflow = jnp.where(seg_rows[inner] == seg_prior, jnp.exp(level), 0.0)
    return jnp.einsum("jh,jhp,jn->hpn", weight, x_rows, b_rows, precision=high), inflow


def tree_allreduce(big, axis, count):
    me = lax.axis_index(axis)
    order = [d for d in (1, 2, 8, 4, 16) if d < count]
    assert sorted(order) == [1 << k for k in range(count.bit_length() - 1)]
    for d in order:
        pairs = [(j, j ^ d) for j in range(count)]
        half = big.shape[0] // 2
        upper = (me // d) % 2
        send = lax.dynamic_slice_in_dim(big, (1 - upper) * half, half, 0)
        keep = lax.dynamic_slice_in_dim(big, upper * half, half, 0)
        big = keep + lax.ppermute(send, axis, pairs)
    for d in reversed(order):
        pairs = [(j, j ^ d) for j in range(count)]
        upper = (me // d) % 2 == 1
        got = lax.ppermute(big, axis, pairs)
        low = jnp.where(upper, got, big)
        high = jnp.where(upper, big, got)
        big = jnp.concatenate([low, high], axis=0)
    return big


def per_device(
    hidden,
    x_weight,
    z_weight,
    bc_weight,
    dt_weight,
    conv_x,
    conv_bc,
    dt_bias,
    decay_rate,
    skip_gain,
    norm_gain,
    out_weight,
    lengths,
    owners,
):
    rows_here = hidden.shape[0]
    width_here = x_weight.shape[1]
    heads_here = dt_bias.shape[0]
    head_width = width_here // heads_here
    seq_count = lax.axis_size("seq")
    my_index = lax.axis_index("seq")
    first_row = my_index * rows_here
    prompt_end = jnp.cumsum(lengths)
    prompt_start = prompt_end - lengths
    positions = first_row + jnp.arange(rows_here, dtype=jnp.int32)
    segment = segment_of(positions, prompt_end)
    piece = lax.all_gather(hidden, "tp", axis=1, tiled=True)
    tp_count = lax.axis_size("tp")
    tp_index = lax.axis_index("tp")
    by_shift = [bc_weight] + [
        lax.ppermute(bc_weight, "tp", [(j, (j + s) % tp_count) for j in range(tp_count)])
        for s in range(1, tp_count)
    ]
    shift_of = (tp_index - jnp.arange(tp_count, dtype=jnp.int32)) % tp_count
    bc_full = jnp.concatenate(
        [jnp.take(jnp.stack(by_shift), shift_of[k], axis=0) for k in range(tp_count)], axis=1
    )

    def take(matrix):
        return jnp.dot(piece, matrix, preferred_element_type=jnp.float32)

    x_acc = take(x_weight)
    z_acc = take(z_weight)
    dt_raw = take(dt_weight)
    bc_acc = take(bc_full)
    x_in = x_acc.astype(jnp.bfloat16)
    z_in = z_acc.astype(jnp.bfloat16)
    bc_in = bc_acc.astype(jnp.bfloat16)
    joined = jnp.concatenate([x_in, bc_in], axis=1)
    earlier = passed_along(joined[rows_here - (KCONV - 1) :], "seq", 1)
    extended = jnp.concatenate([earlier, joined], axis=0)
    seg_ext = jnp.concatenate(
        [
            segment_of(
                first_row - (KCONV - 1) + jnp.arange(KCONV - 1, dtype=jnp.int32), prompt_end
            ),
            segment,
        ]
    )
    kernel = jnp.concatenate([conv_x, conv_bc], axis=1)
    mixed_in = short_conv(extended, seg_ext, kernel)
    x_conv = mixed_in[:, :width_here].astype(jnp.float32).reshape(rows_here, heads_here, head_width)
    b_conv = mixed_in[:, width_here : width_here + NS].astype(jnp.float32)
    c_conv = mixed_in[:, width_here + NS :].astype(jnp.float32)
    step_size = jax.nn.softplus(dt_raw + dt_bias[None, :])
    log_decay = -decay_rate[None, :] * step_size
    device_prior = segment_of(jnp.reshape(first_row - 1, (1,)), prompt_end)[0]
    level = jnp.cumsum(log_decay, axis=0)
    closing = segment[rows_here - 1]
    through = jnp.where(closing == device_prior, jnp.exp(level[rows_here - 1]), 0.0)
    tail = (
        jnp.where(
            (segment == closing)[:, None], jnp.exp(level[rows_here - 1][None, :] - level), 0.0
        )
        * step_size
    )
    local_end = jnp.einsum("jh,jhp,jn->hpn", tail, x_conv, b_conv, precision=high)
    state_cols = head_width * NS
    packed_end = jnp.concatenate(
        [
            local_end.reshape(heads_here, state_cols),
            jnp.broadcast_to(through[:, None], (heads_here, 128)),
        ],
        axis=1,
    )
    gathered = lax.all_gather(packed_end, "seq")
    throughs = gathered[:, :, state_cols]
    source = jnp.arange(seq_count, dtype=jnp.int32)
    last_row = prompt_end - 1
    holder = last_row // rows_here
    keeper = owners[0]

    def entering_of(target):
        between = (source[None, :] > source[:, None]) & (source[None, :] < target)
        factors = jnp.where(between[:, :, None], throughs[None, :, :], 1.0)
        weights = jnp.where((source < target)[:, None], jnp.prod(factors, axis=1), 0.0)
        return jnp.sum(weights[:, :, None] * gathered[:, :, :state_cols], axis=0)

    entering = entering_of(my_index).reshape(heads_here, head_width, NS)
    entering_t = entering_of(holder[keeper])

    blocks = rows_here // GROUP
    state = jnp.zeros((heads_here, head_width, NS), jnp.float32)
    pieces = []
    for blk in range(blocks):
        rows = slice(blk * GROUP, (blk + 1) * GROUP)
        seg_prior = device_prior if blk == 0 else segment[blk * GROUP - 1]
        state, output = advance_block(
            state,
            (
                x_conv[rows],
                b_conv[rows],
                c_conv[rows],
                step_size[rows],
                log_decay[rows],
                segment[rows],
                seg_prior,
            ),
        )
        pieces.append(output)
    ssm = jnp.concatenate(pieces, axis=0)
    inflow = jnp.where((segment == device_prior)[:, None], jnp.exp(level), 0.0)
    ssm = ssm + inflow[:, :, None] * jnp.einsum("in,hpn->ihp", c_conv, entering, precision=high)
    ssm = ssm + skip_gain[None, :, None] * x_conv
    gated_all = ssm.reshape(rows_here, width_here) * jax.nn.silu(z_in.astype(jnp.float32))
    halves = []
    half_rows = rows_here // 2
    for part in range(2):
        gated = gated_all[part * half_rows : (part + 1) * half_rows]
        square_sum = lax.psum(jnp.sum(gated * gated, axis=1), "tp")
        normed = (
            gated * lax.rsqrt(square_sum / DIN + epsilon)[:, None] * norm_gain[None, :]
        ).astype(jnp.bfloat16)
        mixed_cols = lax.psum_scatter(
            lax.dot_general(
                out_weight, normed, (((0,), (1,)), ((), ())), preferred_element_type=jnp.float32
            ).astype(jnp.bfloat16),
            "tp",
            scatter_dimension=0,
            tiled=True,
        )
        halves.append(mixed_cols.T)
    mixed = jnp.concatenate(halves, axis=0)
    present = holder == my_index
    inner = jnp.clip(last_row - first_row, 0, rows_here - 1)

    def finish(prompt_id, inner_row):
        return partial_at(
            device_prior, x_conv, b_conv, step_size, level, segment, inner_row, prompt_id
        )

    partials, factors_at = jax.vmap(finish)(jnp.arange(PROMPTS, dtype=jnp.int32), inner)
    partials = jnp.where(present[:, None, None, None], partials, 0.0)
    factors_at = jnp.where(present[:, None], factors_at, 0.0)

    def edge_of(inner_row, start_row, end_row):
        window = lax.dynamic_slice_in_dim(extended, inner_row + 1, KCONV - 1, 0)
        rows_global = end_row - (KCONV - 2) + jnp.arange(KCONV - 1, dtype=jnp.int32)
        return jnp.where((rows_global >= start_row)[:, None], window, jnp.zeros_like(window))

    edges = jnp.stack(
        [edge_of(inner[r], prompt_start[r], last_row[r]) for r in range(PROMPTS)]
    )
    edges = jnp.where(present[:, None, None], edges, jnp.zeros_like(edges))
    edge_cols = (KCONV - 1) * edges.shape[2]
    factor_hi = factors_at.astype(jnp.bfloat16)
    factor_lo = (factors_at - factor_hi.astype(jnp.float32)).astype(jnp.bfloat16)
    used_cols = heads_here * state_cols + edge_cols + 2 * heads_here
    slot_rows = -(-used_cols // 128)
    total_rows = PROMPTS * slot_rows
    padded_rows = -(-total_rows // (16 * seq_count)) * 16 * seq_count
    payload = jnp.concatenate(
        [
            partials.reshape(PROMPTS, heads_here * state_cols).astype(jnp.bfloat16),
            edges.reshape(PROMPTS, edge_cols),
            factor_hi,
            factor_lo,
            jnp.zeros((PROMPTS, slot_rows * 128 - used_cols), jnp.bfloat16),
        ],
        axis=1,
    ).reshape(total_rows, 128)
    payload = jnp.concatenate(
        [payload, jnp.zeros((padded_rows - total_rows, 128), jnp.bfloat16)], axis=0
    )
    summed = tree_allreduce(payload, "seq", seq_count)
    kept = summed[:total_rows].reshape(PROMPTS, slot_rows * 128)[keeper]
    factor_at = heads_here * state_cols + edge_cols
    factor_kept = kept[factor_at : factor_at + heads_here].astype(jnp.float32) + kept[
        factor_at + heads_here : factor_at + 2 * heads_here
    ].astype(jnp.float32)
    final_flat = (
        factor_kept[:, None] * entering_t
        + kept[: heads_here * state_cols].astype(jnp.float32).reshape(heads_here, state_cols)
    )
    final_state = final_flat.reshape(1, heads_here, head_width, NS)
    kept_edges = kept[heads_here * state_cols : heads_here * state_cols + edge_cols].reshape(
        KCONV - 1, edges.shape[2]
    )
    conv_edge_x = kept_edges[:, :width_here][None]
    conv_edge_bc = kept_edges[:, width_here:][None]
    return (mixed, final_state, conv_edge_x, conv_edge_bc)


def solution(mesh):
    return jax.shard_map(
        per_device,
        mesh=mesh,
        in_specs=(
            P("seq", "tp"),
            P(None, "tp"),
            P(None, "tp"),
            P(None, "tp"),
            P(None, "tp"),
            P(None, "tp"),
            P(),
            P("tp"),
            P("tp"),
            P("tp"),
            P("tp"),
            P("tp", None),
            P(),
            P("seq"),
        ),
        out_specs=(
            P("seq", "tp"),
            P("seq", "tp", None, None),
            P("seq", None, "tp"),
            P("seq", None, None),
        ),
        check_vma=False,
    )
```

```python
import jax
import jax.numpy as jnp
from jax import lax
from jax.sharding import PartitionSpec as P

NS = 128
KCONV = 4
GROUP = 256
PROMPTS = 4
DIN = 4096


highest = lax.Precision.HIGHEST
high = lax.Precision.HIGH
epsilon = 1e-05


def passed_along(block, axis, distance):
    devices = range(lax.axis_size(axis))
    route = [(i - distance, i) for i in devices if i - distance in devices]
    return lax.ppermute(block, axis, route)


def segment_of(positions, prompt_end):
    counted = jnp.sum((positions[:, None] >= prompt_end[None, :]).astype(jnp.int32), axis=1)
    return jnp.where(positions < 0, -1, counted)


def short_conv(extended, seg_ext, kernel):
    taps = kernel.shape[0]
    count = extended.shape[0] - taps + 1
    total = jnp.zeros((count, extended.shape[1]), jnp.float32)
    for offset in range(taps):
        same = (seg_ext[offset : offset + count] == seg_ext[taps - 1 :]).astype(jnp.float32)
        total = (
            total
            + extended[offset : offset + count].astype(jnp.float32)
            * kernel[offset][None, :]
            * same[:, None]
        )
    return jax.nn.silu(total).astype(jnp.bfloat16)


def advance_block(state, block):
    x_blk, b_blk, c_blk, dt_blk, log_blk, seg_blk, seg_prior = block
    length = seg_blk.shape[0]
    acum = jnp.cumsum(log_blk, axis=0)
    index = jnp.arange(length, dtype=jnp.int32)
    keep = (seg_blk[:, None] == seg_blk[None, :]) & (index[:, None] >= index[None, :])
    spread = acum[:, None, :] - acum[None, :, :]
    decay = jnp.where(keep[:, :, None], jnp.exp(jnp.where(keep[:, :, None], spread, 0.0)), 0.0)
    scores = jnp.dot(c_blk.astype(jnp.bfloat16), b_blk.T.astype(jnp.bfloat16), preferred_element_type=jnp.float32)
    mixing = scores[:, :, None] * decay * dt_blk[None, :, :]
    output = jnp.einsum("ijh,jhp->ihp", mixing, x_blk, precision=high)
    inflow = jnp.where((seg_blk == seg_prior)[:, None], jnp.exp(acum), 0.0)
    output = output + inflow[:, :, None] * jnp.einsum(
        "in,hpn->ihp", c_blk, state, precision=high
    )
    closing = seg_blk[length - 1]
    tail = (
        jnp.where((seg_blk == closing)[:, None], jnp.exp(acum[length - 1][None, :] - acum), 0.0)
        * dt_blk
    )
    fresh = jnp.einsum("jh,jhp,jn->hpn", tail, x_blk, b_blk, precision=high)
    carry = jnp.where(closing == seg_prior, jnp.exp(acum[length - 1]), 0.0)
    return carry[:, None, None] * state + fresh, output


def state_at(start_state, seg_prior, x_rows, b_rows, dt_rows, log_rows, seg_rows, inner, prompt):
    acum = jnp.cumsum(log_rows, axis=0)
    level = acum[inner]
    index = jnp.arange(seg_rows.shape[0], dtype=jnp.int32)
    chosen = (seg_rows == prompt) & (index <= inner)
    weight = (
        jnp.where(
            chosen[:, None], jnp.exp(jnp.where(chosen[:, None], level[None, :] - acum, 0.0)), 0.0
        )
        * dt_rows
    )
    inflow = jnp.where(seg_rows[inner] == seg_prior, jnp.exp(level), 0.0)
    return inflow[:, None, None] * start_state + jnp.einsum(
        "jh,jhp,jn->hpn", weight, x_rows, b_rows, precision=highest
    )


def partial_at(seg_prior, x_rows, b_rows, dt_rows, level_rows, seg_rows, inner, prompt):
    level = level_rows[inner]
    index = jnp.arange(seg_rows.shape[0], dtype=jnp.int32)
    chosen = (seg_rows == prompt) & (index <= inner)
    weight = (
        jnp.where(
            chosen[:, None],
            jnp.exp(jnp.where(chosen[:, None], level[None, :] - level_rows, 0.0)),
            0.0,
        )
        * dt_rows
    )
    inflow = jnp.where(seg_rows[inner] == seg_prior, jnp.exp(level), 0.0)
    return jnp.einsum("jh,jhp,jn->hpn", weight, x_rows, b_rows, precision=high), inflow


def tree_allreduce(big, axis, count):
    me = lax.axis_index(axis)
    order = [d for d in (1, 2, 8, 4, 16) if d < count]
    assert sorted(order) == [1 << k for k in range(count.bit_length() - 1)]
    for d in order:
        pairs = [(j, j ^ d) for j in range(count)]
        half = big.shape[0] // 2
        upper = (me // d) % 2
        send = lax.dynamic_slice_in_dim(big, (1 - upper) * half, half, 0)
        keep = lax.dynamic_slice_in_dim(big, upper * half, half, 0)
        big = keep + lax.ppermute(send, axis, pairs)
    for d in reversed(order):
        pairs = [(j, j ^ d) for j in range(count)]
        upper = (me // d) % 2 == 1
        got = lax.ppermute(big, axis, pairs)
        low = jnp.where(upper, got, big)
        high = jnp.where(upper, big, got)
        big = jnp.concatenate([low, high], axis=0)
    return big


def per_device(
    hidden,
    x_weight,
    z_weight,
    bc_weight,
    dt_weight,
    conv_x,
    conv_bc,
    dt_bias,
    decay_rate,
    skip_gain,
    norm_gain,
    out_weight,
    lengths,
    owners,
):
    rows_here = hidden.shape[0]
    width_here = x_weight.shape[1]
    heads_here = dt_bias.shape[0]
    head_width = width_here // heads_here
    seq_count = lax.axis_size("seq")
    my_index = lax.axis_index("seq")
    first_row = my_index * rows_here
    prompt_end = jnp.cumsum(lengths)
    prompt_start = prompt_end - lengths
    positions = first_row + jnp.arange(rows_here, dtype=jnp.int32)
    segment = segment_of(positions, prompt_end)
    piece = lax.all_gather(hidden, "tp", axis=1, tiled=True)
    tp_count = lax.axis_size("tp")
    tp_index = lax.axis_index("tp")
    by_shift = [bc_weight] + [
        lax.ppermute(bc_weight, "tp", [(j, (j + s) % tp_count) for j in range(tp_count)])
        for s in range(1, tp_count)
    ]
    shift_of = (tp_index - jnp.arange(tp_count, dtype=jnp.int32)) % tp_count
    bc_full = jnp.concatenate(
        [jnp.take(jnp.stack(by_shift), shift_of[k], axis=0) for k in range(tp_count)], axis=1
    )

    def take(matrix):
        return jnp.dot(piece, matrix, preferred_element_type=jnp.float32)

    x_acc = take(x_weight)
    z_acc = take(z_weight)
    dt_raw = take(dt_weight)
    bc_acc = take(bc_full)
    x_in = x_acc.astype(jnp.bfloat16)
    z_in = z_acc.astype(jnp.bfloat16)
    bc_in = bc_acc.astype(jnp.bfloat16)
    joined = jnp.concatenate([x_in, bc_in], axis=1)
    earlier = passed_along(joined[rows_here - (KCONV - 1) :], "seq", 1)
    extended = jnp.concatenate([earlier, joined], axis=0)
    seg_ext = jnp.concatenate(
        [
            segment_of(
                first_row - (KCONV - 1) + jnp.arange(KCONV - 1, dtype=jnp.int32), prompt_end
            ),
            segment,
        ]
    )
    kernel = jnp.concatenate([conv_x, conv_bc], axis=1)
    mixed_in = short_conv(extended, seg_ext, kernel)
    x_conv = mixed_in[:, :width_here].astype(jnp.float32).reshape(rows_here, heads_here, head_width)
    b_conv = mixed_in[:, width_here : width_here + NS].astype(jnp.float32)
    c_conv = mixed_in[:, width_here + NS :].astype(jnp.float32)
    step_size = jax.nn.softplus(dt_raw + dt_bias[None, :])
    log_decay = -decay_rate[None, :] * step_size
    device_prior = segment_of(jnp.reshape(first_row - 1, (1,)), prompt_end)[0]
    level = jnp.cumsum(log_decay, axis=0)
    closing = segment[rows_here - 1]
    through = jnp.where(closing == device_prior, jnp.exp(level[rows_here - 1]), 0.0)
    tail = (
        jnp.where(
            (segment == closing)[:, None], jnp.exp(level[rows_here - 1][None, :] - level), 0.0
        )
        * step_size
    )
    local_end = jnp.einsum("jh,jhp,jn->hpn", tail, x_conv, b_conv, precision=high)
    state_cols = head_width * NS
    packed_end = jnp.concatenate(
        [
            local_end.reshape(heads_here, state_cols),
            jnp.broadcast_to(through[:, None], (heads_here, 128)),
        ],
        axis=1,
    )
    gathered = lax.all_gather(packed_end, "seq")
    throughs = gathered[:, :, state_cols]
    source = jnp.arange(seq_count, dtype=jnp.int32)
    last_row = prompt_end - 1
    holder = last_row // rows_here
    keeper = owners[0]

    def entering_of(target):
        between = (source[None, :] > source[:, None]) & (source[None, :] < target)
        factors = jnp.where(between[:, :, None], throughs[None, :, :], 1.0)
        weights = jnp.where((source < target)[:, None], jnp.prod(factors, axis=1), 0.0)
        return jnp.sum(weights[:, :, None] * gathered[:, :, :state_cols], axis=0)

    entering = entering_of(my_index).reshape(heads_here, head_width, NS)
    entering_t = entering_of(holder[keeper])

    blocks = rows_here // GROUP
    state = jnp.zeros((heads_here, head_width, NS), jnp.float32)
    pieces = []
    for blk in range(blocks):
        rows = slice(blk * GROUP, (blk + 1) * GROUP)
        seg_prior = device_prior if blk == 0 else segment[blk * GROUP - 1]
        state, output = advance_block(
            state,
            (
                x_conv[rows],
                b_conv[rows],
                c_conv[rows],
                step_size[rows],
                log_decay[rows],
                segment[rows],
                seg_prior,
            ),
        )
        pieces.append(output)
    ssm = jnp.concatenate(pieces, axis=0)
    inflow = jnp.where((segment == device_prior)[:, None], jnp.exp(level), 0.0)
    ssm = ssm + inflow[:, :, None] * jnp.einsum("in,hpn->ihp", c_conv, entering, precision=high)
    ssm = ssm + skip_gain[None, :, None] * x_conv
    gated_all = ssm.reshape(rows_here, width_here) * jax.nn.silu(z_in.astype(jnp.float32))
    halves = []
    half_rows = rows_here // 2
    for part in range(2):
        gated = gated_all[part * half_rows : (part + 1) * half_rows]
        square_sum = lax.psum(jnp.sum(gated * gated, axis=1), "tp")
        scaled = (gated * norm_gain[None, :]).astype(jnp.bfloat16)
        mixed_cols = lax.psum_scatter(
            lax.dot_general(
                out_weight, scaled, (((0,), (1,)), ((), ())), preferred_element_type=jnp.float32
            ).astype(jnp.bfloat16),
            "tp",
            scatter_dimension=0,
            tiled=True,
        )
        row_scale = lax.rsqrt(square_sum / DIN + epsilon)
        halves.append((mixed_cols.astype(jnp.float32) * row_scale[None, :]).T.astype(jnp.bfloat16))
    mixed = jnp.concatenate(halves, axis=0)
    present = holder == my_index
    inner = jnp.clip(last_row - first_row, 0, rows_here - 1)

    def finish(prompt_id, inner_row):
        return partial_at(
            device_prior, x_conv, b_conv, step_size, level, segment, inner_row, prompt_id
        )

    partials, factors_at = jax.vmap(finish)(jnp.arange(PROMPTS, dtype=jnp.int32), inner)
    partials = jnp.where(present[:, None, None, None], partials, 0.0)
    factors_at = jnp.where(present[:, None], factors_at, 0.0)

    def edge_of(inner_row, start_row, end_row):
        window = lax.dynamic_slice_in_dim(extended, inner_row + 1, KCONV - 1, 0)
        rows_global = end_row - (KCONV - 2) + jnp.arange(KCONV - 1, dtype=jnp.int32)
        return jnp.where((rows_global >= start_row)[:, None], window, jnp.zeros_like(window))

    edges = jnp.stack(
        [edge_of(inner[r], prompt_start[r], last_row[r]) for r in range(PROMPTS)]
    )
    edges = jnp.where(present[:, None, None], edges, jnp.zeros_like(edges))
    edge_cols = (KCONV - 1) * edges.shape[2]
    factor_hi = factors_at.astype(jnp.bfloat16)
    factor_lo = (factors_at - factor_hi.astype(jnp.float32)).astype(jnp.bfloat16)
    used_cols = heads_here * state_cols + edge_cols + 2 * heads_here
    slot_rows = -(-used_cols // 128)
    total_rows = PROMPTS * slot_rows
    padded_rows = -(-total_rows // (16 * seq_count)) * 16 * seq_count
    payload = jnp.concatenate(
        [
            partials.reshape(PROMPTS, heads_here * state_cols).astype(jnp.bfloat16),
            edges.reshape(PROMPTS, edge_cols),
            factor_hi,
            factor_lo,
            jnp.zeros((PROMPTS, slot_rows * 128 - used_cols), jnp.bfloat16),
        ],
        axis=1,
    ).reshape(total_rows, 128)
    payload = jnp.concatenate(
        [payload, jnp.zeros((padded_rows - total_rows, 128), jnp.bfloat16)], axis=0
    )
    summed = tree_allreduce(payload, "seq", seq_count)
    kept = summed[:total_rows].reshape(PROMPTS, slot_rows * 128)[keeper]
    factor_at = heads_here * state_cols + edge_cols
    factor_kept = kept[factor_at : factor_at + heads_here].astype(jnp.float32) + kept[
        factor_at + heads_here : factor_at + 2 * heads_here
    ].astype(jnp.float32)
    final_flat = (
        factor_kept[:, None] * entering_t
        + kept[: heads_here * state_cols].astype(jnp.float32).reshape(heads_here, state_cols)
    )
    final_state = final_flat.reshape(1, heads_here, head_width, NS)
    kept_edges = kept[heads_here * state_cols : heads_here * state_cols + edge_cols].reshape(
        KCONV - 1, edges.shape[2]
    )
    conv_edge_x = kept_edges[:, :width_here][None]
    conv_edge_bc = kept_edges[:, width_here:][None]
    return (mixed, final_state, conv_edge_x, conv_edge_bc)


def solution(mesh):
    return jax.shard_map(
        per_device,
        mesh=mesh,
        in_specs=(
            P("seq", "tp"),
            P(None, "tp"),
            P(None, "tp"),
            P(None, "tp"),
            P(None, "tp"),
            P(None, "tp"),
            P(),
            P("tp"),
            P("tp"),
            P("tp"),
            P("tp"),
            P("tp", None),
            P(),
            P("seq"),
        ),
        out_specs=(
            P("seq", "tp"),
            P("seq", "tp", None, None),
            P("seq", None, "tp"),
            P("seq", None, None),
        ),
        check_vma=False,
    )
```

```python
import jax
import jax.numpy as jnp
from jax import lax
from jax.sharding import PartitionSpec as P

NS = 128
KCONV = 4
GROUP = 256
PROMPTS = 4
DIN = 4096


highest = lax.Precision.HIGHEST
high = lax.Precision.HIGH
epsilon = 1e-05


def passed_along(block, axis, distance):
    devices = range(lax.axis_size(axis))
    route = [(i - distance, i) for i in devices if i - distance in devices]
    return lax.ppermute(block, axis, route)


def segment_of(positions, prompt_end):
    counted = jnp.sum((positions[:, None] >= prompt_end[None, :]).astype(jnp.int32), axis=1)
    return jnp.where(positions < 0, -1, counted)


def short_conv(extended, seg_ext, kernel):
    taps = kernel.shape[0]
    count = extended.shape[0] - taps + 1
    total = jnp.zeros((count, extended.shape[1]), jnp.float32)
    for offset in range(taps):
        same = (seg_ext[offset : offset + count] == seg_ext[taps - 1 :]).astype(jnp.float32)
        total = (
            total
            + extended[offset : offset + count].astype(jnp.float32)
            * kernel[offset][None, :]
            * same[:, None]
        )
    return jax.nn.silu(total).astype(jnp.bfloat16)


def advance_block(state, block):
    x_blk, b_blk, c_blk, dt_blk, log_blk, seg_blk, seg_prior = block
    length = seg_blk.shape[0]
    acum = jnp.cumsum(log_blk, axis=0)
    index = jnp.arange(length, dtype=jnp.int32)
    keep = (seg_blk[:, None] == seg_blk[None, :]) & (index[:, None] >= index[None, :])
    spread = acum[:, None, :] - acum[None, :, :]
    decay = jnp.where(keep[:, :, None], jnp.exp(jnp.where(keep[:, :, None], spread, 0.0)), 0.0)
    scores = jnp.dot(c_blk.astype(jnp.bfloat16), b_blk.T.astype(jnp.bfloat16), preferred_element_type=jnp.float32)
    mixing = scores[:, :, None] * decay * dt_blk[None, :, :]
    output = jnp.einsum("ijh,jhp->ihp", mixing, x_blk, precision=high)
    inflow = jnp.where((seg_blk == seg_prior)[:, None], jnp.exp(acum), 0.0)
    output = output + inflow[:, :, None] * jnp.einsum(
        "in,hpn->ihp", c_blk, state, precision=high
    )
    closing = seg_blk[length - 1]
    tail = (
        jnp.where((seg_blk == closing)[:, None], jnp.exp(acum[length - 1][None, :] - acum), 0.0)
        * dt_blk
    )
    fresh = jnp.einsum("jh,jhp,jn->hpn", tail, x_blk, b_blk, precision=high)
    carry = jnp.where(closing == seg_prior, jnp.exp(acum[length - 1]), 0.0)
    return carry[:, None, None] * state + fresh, output


def state_at(start_state, seg_prior, x_rows, b_rows, dt_rows, log_rows, seg_rows, inner, prompt):
    acum = jnp.cumsum(log_rows, axis=0)
    level = acum[inner]
    index = jnp.arange(seg_rows.shape[0], dtype=jnp.int32)
    chosen = (seg_rows == prompt) & (index <= inner)
    weight = (
        jnp.where(
            chosen[:, None], jnp.exp(jnp.where(chosen[:, None], level[None, :] - acum, 0.0)), 0.0
        )
        * dt_rows
    )
    inflow = jnp.where(seg_rows[inner] == seg_prior, jnp.exp(level), 0.0)
    return inflow[:, None, None] * start_state + jnp.einsum(
        "jh,jhp,jn->hpn", weight, x_rows, b_rows, precision=highest
    )


def partial_at(seg_prior, x_rows, b_rows, dt_rows, level_rows, seg_rows, inner, prompt):
    level = level_rows[inner]
    index = jnp.arange(seg_rows.shape[0], dtype=jnp.int32)
    chosen = (seg_rows == prompt) & (index <= inner)
    weight = (
        jnp.where(
            chosen[:, None],
            jnp.exp(jnp.where(chosen[:, None], level[None, :] - level_rows, 0.0)),
            0.0,
        )
        * dt_rows
    )
    inflow = jnp.where(seg_rows[inner] == seg_prior, jnp.exp(level), 0.0)
    return jnp.einsum("jh,jhp,jn->hpn", weight, x_rows, b_rows, precision=high), inflow


def tree_allreduce(big, axis, count):
    me = lax.axis_index(axis)
    order = [d for d in (1, 2, 8, 4, 16) if d < count]
    assert sorted(order) == [1 << k for k in range(count.bit_length() - 1)]
    for d in order:
        pairs = [(j, j ^ d) for j in range(count)]
        half = big.shape[0] // 2
        upper = (me // d) % 2
        send = lax.dynamic_slice_in_dim(big, (1 - upper) * half, half, 0)
        keep = lax.dynamic_slice_in_dim(big, upper * half, half, 0)
        big = keep + lax.ppermute(send, axis, pairs)
    bits = len(order)
    gathered = lax.all_gather(big, axis).reshape([2] * bits + list(big.shape))
    axes = [bits - d.bit_length() for d in order] + [bits + k for k in range(big.ndim)]
    return jnp.transpose(gathered, axes).reshape((count * big.shape[0],) + big.shape[1:])


def per_device(
    hidden,
    x_weight,
    z_weight,
    bc_weight,
    dt_weight,
    conv_x,
    conv_bc,
    dt_bias,
    decay_rate,
    skip_gain,
    norm_gain,
    out_weight,
    lengths,
    owners,
):
    rows_here = hidden.shape[0]
    width_here = x_weight.shape[1]
    heads_here = dt_bias.shape[0]
    head_width = width_here // heads_here
    seq_count = lax.axis_size("seq")
    my_index = lax.axis_index("seq")
    first_row = my_index * rows_here
    prompt_end = jnp.cumsum(lengths)
    prompt_start = prompt_end - lengths
    positions = first_row + jnp.arange(rows_here, dtype=jnp.int32)
    segment = segment_of(positions, prompt_end)
    piece = lax.all_gather(hidden, "tp", axis=1, tiled=True)
    tp_count = lax.axis_size("tp")
    tp_index = lax.axis_index("tp")
    by_shift = [bc_weight] + [
        lax.ppermute(bc_weight, "tp", [(j, (j + s) % tp_count) for j in range(tp_count)])
        for s in range(1, tp_count)
    ]
    shift_of = (tp_index - jnp.arange(tp_count, dtype=jnp.int32)) % tp_count
    bc_full = jnp.concatenate(
        [jnp.take(jnp.stack(by_shift), shift_of[k], axis=0) for k in range(tp_count)], axis=1
    )

    def take(matrix):
        return jnp.dot(piece, matrix, preferred_element_type=jnp.float32)

    x_acc = take(x_weight)
    z_acc = take(z_weight)
    dt_raw = take(dt_weight)
    bc_acc = take(bc_full)
    x_in = x_acc.astype(jnp.bfloat16)
    z_in = z_acc.astype(jnp.bfloat16)
    bc_in = bc_acc.astype(jnp.bfloat16)
    joined = jnp.concatenate([x_in, bc_in], axis=1)
    earlier = passed_along(joined[rows_here - (KCONV - 1) :], "seq", 1)
    extended = jnp.concatenate([earlier, joined], axis=0)
    seg_ext = jnp.concatenate(
        [
            segment_of(
                first_row - (KCONV - 1) + jnp.arange(KCONV - 1, dtype=jnp.int32), prompt_end
            ),
            segment,
        ]
    )
    kernel = jnp.concatenate([conv_x, conv_bc], axis=1)
    mixed_in = short_conv(extended, seg_ext, kernel)
    x_conv = mixed_in[:, :width_here].astype(jnp.float32).reshape(rows_here, heads_here, head_width)
    b_conv = mixed_in[:, width_here : width_here + NS].astype(jnp.float32)
    c_conv = mixed_in[:, width_here + NS :].astype(jnp.float32)
    step_size = jax.nn.softplus(dt_raw + dt_bias[None, :])
    log_decay = -decay_rate[None, :] * step_size
    device_prior = segment_of(jnp.reshape(first_row - 1, (1,)), prompt_end)[0]
    level = jnp.cumsum(log_decay, axis=0)
    closing = segment[rows_here - 1]
    through = jnp.where(closing == device_prior, jnp.exp(level[rows_here - 1]), 0.0)
    tail = (
        jnp.where(
            (segment == closing)[:, None], jnp.exp(level[rows_here - 1][None, :] - level), 0.0
        )
        * step_size
    )
    local_end = jnp.einsum("jh,jhp,jn->hpn", tail, x_conv, b_conv, precision=high)
    state_cols = head_width * NS
    packed_end = jnp.concatenate(
        [
            local_end.reshape(heads_here, state_cols),
            jnp.broadcast_to(through[:, None], (heads_here, 128)),
        ],
        axis=1,
    )
    gathered = lax.all_gather(packed_end, "seq")
    throughs = gathered[:, :, state_cols]
    source = jnp.arange(seq_count, dtype=jnp.int32)
    last_row = prompt_end - 1
    holder = last_row // rows_here
    keeper = owners[0]

    def entering_of(target):
        between = (source[None, :] > source[:, None]) & (source[None, :] < target)
        factors = jnp.where(between[:, :, None], throughs[None, :, :], 1.0)
        weights = jnp.where((source < target)[:, None], jnp.prod(factors, axis=1), 0.0)
        return jnp.sum(weights[:, :, None] * gathered[:, :, :state_cols], axis=0)

    entering = entering_of(my_index).reshape(heads_here, head_width, NS)
    entering_t = entering_of(holder[keeper])

    blocks = rows_here // GROUP
    state = jnp.zeros((heads_here, head_width, NS), jnp.float32)
    pieces = []
    for blk in range(blocks):
        rows = slice(blk * GROUP, (blk + 1) * GROUP)
        seg_prior = device_prior if blk == 0 else segment[blk * GROUP - 1]
        state, output = advance_block(
            state,
            (
                x_conv[rows],
                b_conv[rows],
                c_conv[rows],
                step_size[rows],
                log_decay[rows],
                segment[rows],
                seg_prior,
            ),
        )
        pieces.append(output)
    ssm = jnp.concatenate(pieces, axis=0)
    inflow = jnp.where((segment == device_prior)[:, None], jnp.exp(level), 0.0)
    ssm = ssm + inflow[:, :, None] * jnp.einsum("in,hpn->ihp", c_conv, entering, precision=high)
    ssm = ssm + skip_gain[None, :, None] * x_conv
    gated_all = ssm.reshape(rows_here, width_here) * jax.nn.silu(z_in.astype(jnp.float32))
    halves = []
    half_rows = rows_here // 2
    for part in range(2):
        gated = gated_all[part * half_rows : (part + 1) * half_rows]
        square_sum = lax.psum(jnp.sum(gated * gated, axis=1), "tp")
        normed = (
            gated * lax.rsqrt(square_sum / DIN + epsilon)[:, None] * norm_gain[None, :]
        ).astype(jnp.bfloat16)
        mixed_cols = lax.psum_scatter(
            lax.dot_general(
                out_weight, normed, (((0,), (1,)), ((), ())), preferred_element_type=jnp.float32
            ).astype(jnp.bfloat16),
            "tp",
            scatter_dimension=0,
            tiled=True,
        )
        halves.append(mixed_cols.T)
    mixed = jnp.concatenate(halves, axis=0)
    present = holder == my_index
    inner = jnp.clip(last_row - first_row, 0, rows_here - 1)

    def finish(prompt_id, inner_row):
        return partial_at(
            device_prior, x_conv, b_conv, step_size, level, segment, inner_row, prompt_id
        )

    partials, factors_at = jax.vmap(finish)(jnp.arange(PROMPTS, dtype=jnp.int32), inner)
    partials = jnp.where(present[:, None, None, None], partials, 0.0)
    factors_at = jnp.where(present[:, None], factors_at, 0.0)

    def edge_of(inner_row, start_row, end_row):
        window = lax.dynamic_slice_in_dim(extended, inner_row + 1, KCONV - 1, 0)
        rows_global = end_row - (KCONV - 2) + jnp.arange(KCONV - 1, dtype=jnp.int32)
        return jnp.where((rows_global >= start_row)[:, None], window, jnp.zeros_like(window))

    edges = jnp.stack(
        [edge_of(inner[r], prompt_start[r], last_row[r]) for r in range(PROMPTS)]
    )
    edges = jnp.where(present[:, None, None], edges, jnp.zeros_like(edges))
    edge_cols = (KCONV - 1) * edges.shape[2]
    factor_hi = factors_at.astype(jnp.bfloat16)
    factor_lo = (factors_at - factor_hi.astype(jnp.float32)).astype(jnp.bfloat16)
    used_cols = heads_here * state_cols + edge_cols + 2 * heads_here
    slot_rows = -(-used_cols // 128)
    total_rows = PROMPTS * slot_rows
    padded_rows = -(-total_rows // (16 * seq_count)) * 16 * seq_count
    payload = jnp.concatenate(
        [
            partials.reshape(PROMPTS, heads_here * state_cols).astype(jnp.bfloat16),
            edges.reshape(PROMPTS, edge_cols),
            factor_hi,
            factor_lo,
            jnp.zeros((PROMPTS, slot_rows * 128 - used_cols), jnp.bfloat16),
        ],
        axis=1,
    ).reshape(total_rows, 128)
    payload = jnp.concatenate(
        [payload, jnp.zeros((padded_rows - total_rows, 128), jnp.bfloat16)], axis=0
    )
    summed = tree_allreduce(payload, "seq", seq_count)
    kept = summed[:total_rows].reshape(PROMPTS, slot_rows * 128)[keeper]
    factor_at = heads_here * state_cols + edge_cols
    factor_kept = kept[factor_at : factor_at + heads_here].astype(jnp.float32) + kept[
        factor_at + heads_here : factor_at + 2 * heads_here
    ].astype(jnp.float32)
    final_flat = (
        factor_kept[:, None] * entering_t
        + kept[: heads_here * state_cols].astype(jnp.float32).reshape(heads_here, state_cols)
    )
    final_state = final_flat.reshape(1, heads_here, head_width, NS)
    kept_edges = kept[heads_here * state_cols : heads_here * state_cols + edge_cols].reshape(
        KCONV - 1, edges.shape[2]
    )
    conv_edge_x = kept_edges[:, :width_here][None]
    conv_edge_bc = kept_edges[:, width_here:][None]
    return (mixed, final_state, conv_edge_x, conv_edge_bc)


def solution(mesh):
    return jax.shard_map(
        per_device,
        mesh=mesh,
        in_specs=(
            P("seq", "tp"),
            P(None, "tp"),
            P(None, "tp"),
            P(None, "tp"),
            P(None, "tp"),
            P(None, "tp"),
            P(),
            P("tp"),
            P("tp"),
            P("tp"),
            P("tp"),
            P("tp", None),
            P(),
            P("seq"),
        ),
        out_specs=(
            P("seq", "tp"),
            P("seq", "tp", None, None),
            P("seq", None, "tp"),
            P("seq", None, None),
        ),
        check_vma=False,
    )
```

```python
import jax
import jax.numpy as jnp
from jax import lax
from jax.sharding import PartitionSpec as P

NS = 128
KCONV = 4
GROUP = 256
PROMPTS = 4
DIN = 4096


highest = lax.Precision.HIGHEST
high = lax.Precision.HIGH
epsilon = 1e-05


def passed_along(block, axis, distance):
    devices = range(lax.axis_size(axis))
    route = [(i - distance, i) for i in devices if i - distance in devices]
    return lax.ppermute(block, axis, route)


def segment_of(positions, prompt_end):
    counted = jnp.sum((positions[:, None] >= prompt_end[None, :]).astype(jnp.int32), axis=1)
    return jnp.where(positions < 0, -1, counted)


def short_conv(extended, seg_ext, kernel):
    taps = kernel.shape[0]
    count = extended.shape[0] - taps + 1
    total = jnp.zeros((count, extended.shape[1]), jnp.float32)
    for offset in range(taps):
        same = (seg_ext[offset : offset + count] == seg_ext[taps - 1 :]).astype(jnp.float32)
        total = (
            total
            + extended[offset : offset + count].astype(jnp.float32)
            * kernel[offset][None, :]
            * same[:, None]
        )
    return jax.nn.silu(total).astype(jnp.bfloat16)


def advance_block(state, block):
    x_blk, b_blk, c_blk, dt_blk, log_blk, seg_blk, seg_prior = block
    length = seg_blk.shape[0]
    acum = jnp.cumsum(log_blk, axis=0)
    index = jnp.arange(length, dtype=jnp.int32)
    keep = (seg_blk[:, None] == seg_blk[None, :]) & (index[:, None] >= index[None, :])
    spread = acum[:, None, :] - acum[None, :, :]
    decay = jnp.where(keep[:, :, None], jnp.exp(jnp.where(keep[:, :, None], spread, 0.0)), 0.0)
    scores = jnp.dot(c_blk.astype(jnp.bfloat16), b_blk.T.astype(jnp.bfloat16), preferred_element_type=jnp.float32)
    mixing = scores[:, :, None] * decay * dt_blk[None, :, :]
    output = jnp.einsum("ijh,jhp->ihp", mixing, x_blk, precision=high)
    inflow = jnp.where((seg_blk == seg_prior)[:, None], jnp.exp(acum), 0.0)
    output = output + inflow[:, :, None] * jnp.einsum(
        "in,hpn->ihp", c_blk, state, precision=high
    )
    closing = seg_blk[length - 1]
    tail = (
        jnp.where((seg_blk == closing)[:, None], jnp.exp(acum[length - 1][None, :] - acum), 0.0)
        * dt_blk
    )
    fresh = jnp.einsum("jh,jhp,jn->hpn", tail, x_blk, b_blk, precision=high)
    carry = jnp.where(closing == seg_prior, jnp.exp(acum[length - 1]), 0.0)
    return carry[:, None, None] * state + fresh, output


def state_at(start_state, seg_prior, x_rows, b_rows, dt_rows, log_rows, seg_rows, inner, prompt):
    acum = jnp.cumsum(log_rows, axis=0)
    level = acum[inner]
    index = jnp.arange(seg_rows.shape[0], dtype=jnp.int32)
    chosen = (seg_rows == prompt) & (index <= inner)
    weight = (
        jnp.where(
            chosen[:, None], jnp.exp(jnp.where(chosen[:, None], level[None, :] - acum, 0.0)), 0.0
        )
        * dt_rows
    )
    inflow = jnp.where(seg_rows[inner] == seg_prior, jnp.exp(level), 0.0)
    return inflow[:, None, None] * start_state + jnp.einsum(
        "jh,jhp,jn->hpn", weight, x_rows, b_rows, precision=highest
    )


def partial_at(seg_prior, x_rows, b_rows, dt_rows, level_rows, seg_rows, inner, prompt):
    level = level_rows[inner]
    index = jnp.arange(seg_rows.shape[0], dtype=jnp.int32)
    chosen = (seg_rows == prompt) & (index <= inner)
    weight = (
        jnp.where(
            chosen[:, None],
            jnp.exp(jnp.where(chosen[:, None], level[None, :] - level_rows, 0.0)),
            0.0,
        )
        * dt_rows
    )
    inflow = jnp.where(seg_rows[inner] == seg_prior, jnp.exp(level), 0.0)
    return jnp.einsum("jh,jhp,jn->hpn", weight, x_rows, b_rows, precision=high), inflow


def tree_allreduce(big, axis, count):
    me = lax.axis_index(axis)
    order = [d for d in (1, 2, 8, 4, 16) if d < count]
    assert sorted(order) == [1 << k for k in range(count.bit_length() - 1)]
    for d in order:
        pairs = [(j, j ^ d) for j in range(count)]
        half = big.shape[0] // 2
        upper = (me // d) % 2
        send = lax.dynamic_slice_in_dim(big, (1 - upper) * half, half, 0)
        keep = lax.dynamic_slice_in_dim(big, upper * half, half, 0)
        big = keep + lax.ppermute(send, axis, pairs)
    for d in reversed(order):
        pairs = [(j, j ^ d) for j in range(count)]
        upper = (me // d) % 2 == 1
        got = lax.ppermute(big, axis, pairs)
        low = jnp.where(upper, got, big)
        high = jnp.where(upper, big, got)
        big = jnp.concatenate([low, high], axis=0)
    return big


def per_device(
    hidden,
    x_weight,
    z_weight,
    bc_weight,
    dt_weight,
    conv_x,
    conv_bc,
    dt_bias,
    decay_rate,
    skip_gain,
    norm_gain,
    out_weight,
    lengths,
    owners,
):
    rows_here = hidden.shape[0]
    width_here = x_weight.shape[1]
    heads_here = dt_bias.shape[0]
    head_width = width_here // heads_here
    seq_count = lax.axis_size("seq")
    my_index = lax.axis_index("seq")
    first_row = my_index * rows_here
    prompt_end = jnp.cumsum(lengths)
    prompt_start = prompt_end - lengths
    positions = first_row + jnp.arange(rows_here, dtype=jnp.int32)
    segment = segment_of(positions, prompt_end)
    tp_count = lax.axis_size("tp")
    tp_index = lax.axis_index("tp")
    split_row = rows_here // 2
    top = lax.all_gather(hidden[:split_row], "tp", axis=1, tiled=True)
    low_half = hidden[split_row:]
    low_by_shift = [low_half] + [
        lax.ppermute(low_half, "tp", [(j, (j + s) % tp_count) for j in range(tp_count)])
        for s in range(1, tp_count)
    ]
    low_order = (tp_index - jnp.arange(tp_count, dtype=jnp.int32)) % tp_count
    bottom = jnp.concatenate(
        [jnp.take(jnp.stack(low_by_shift), low_order[k], axis=0) for k in range(tp_count)],
        axis=1,
    )
    piece = jnp.concatenate([top, bottom], axis=0)
    by_shift = [bc_weight] + [
        lax.ppermute(bc_weight, "tp", [(j, (j + s) % tp_count) for j in range(tp_count)])
        for s in range(1, tp_count)
    ]
    shift_of = (tp_index - jnp.arange(tp_count, dtype=jnp.int32)) % tp_count
    bc_full = jnp.concatenate(
        [jnp.take(jnp.stack(by_shift), shift_of[k], axis=0) for k in range(tp_count)], axis=1
    )

    def take(matrix):
        return jnp.dot(piece, matrix, preferred_element_type=jnp.float32)

    x_acc = take(x_weight)
    z_acc = take(z_weight)
    dt_raw = take(dt_weight)
    bc_acc = take(bc_full)
    x_in = x_acc.astype(jnp.bfloat16)
    z_in = z_acc.astype(jnp.bfloat16)
    bc_in = bc_acc.astype(jnp.bfloat16)
    joined = jnp.concatenate([x_in, bc_in], axis=1)
    earlier = passed_along(joined[rows_here - (KCONV - 1) :], "seq", 1)
    extended = jnp.concatenate([earlier, joined], axis=0)
    seg_ext = jnp.concatenate(
        [
            segment_of(
                first_row - (KCONV - 1) + jnp.arange(KCONV - 1, dtype=jnp.int32), prompt_end
            ),
            segment,
        ]
    )
    kernel = jnp.concatenate([conv_x, conv_bc], axis=1)
    mixed_in = short_conv(extended, seg_ext, kernel)
    x_conv = mixed_in[:, :width_here].astype(jnp.float32).reshape(rows_here, heads_here, head_width)
    b_conv = mixed_in[:, width_here : width_here + NS].astype(jnp.float32)
    c_conv = mixed_in[:, width_here + NS :].astype(jnp.float32)
    step_size = jax.nn.softplus(dt_raw + dt_bias[None, :])
    log_decay = -decay_rate[None, :] * step_size
    device_prior = segment_of(jnp.reshape(first_row - 1, (1,)), prompt_end)[0]
    level = jnp.cumsum(log_decay, axis=0)
    closing = segment[rows_here - 1]
    through = jnp.where(closing == device_prior, jnp.exp(level[rows_here - 1]), 0.0)
    tail = (
        jnp.where(
            (segment == closing)[:, None], jnp.exp(level[rows_here - 1][None, :] - level), 0.0
        )
        * step_size
    )
    local_end = jnp.einsum("jh,jhp,jn->hpn", tail, x_conv, b_conv, precision=high)
    state_cols = head_width * NS
    packed_end = jnp.concatenate(
        [
            local_end.reshape(heads_here, state_cols),
            jnp.broadcast_to(through[:, None], (heads_here, 128)),
        ],
        axis=1,
    )
    gathered = lax.all_gather(packed_end, "seq")
    throughs = gathered[:, :, state_cols]
    source = jnp.arange(seq_count, dtype=jnp.int32)
    last_row = prompt_end - 1
    holder = last_row // rows_here
    keeper = owners[0]

    def entering_of(target):
        between = (source[None, :] > source[:, None]) & (source[None, :] < target)
        factors = jnp.where(between[:, :, None], throughs[None, :, :], 1.0)
        weights = jnp.where((source < target)[:, None], jnp.prod(factors, axis=1), 0.0)
        return jnp.sum(weights[:, :, None] * gathered[:, :, :state_cols], axis=0)

    entering = entering_of(my_index).reshape(heads_here, head_width, NS)
    entering_t = entering_of(holder[keeper])

    blocks = rows_here // GROUP
    state = jnp.zeros((heads_here, head_width, NS), jnp.float32)
    pieces = []
    for blk in range(blocks):
        rows = slice(blk * GROUP, (blk + 1) * GROUP)
        seg_prior = device_prior if blk == 0 else segment[blk * GROUP - 1]
        state, output = advance_block(
            state,
            (
                x_conv[rows],
                b_conv[rows],
                c_conv[rows],
                step_size[rows],
                log_decay[rows],
                segment[rows],
                seg_prior,
            ),
        )
        pieces.append(output)
    ssm = jnp.concatenate(pieces, axis=0)
    inflow = jnp.where((segment == device_prior)[:, None], jnp.exp(level), 0.0)
    ssm = ssm + inflow[:, :, None] * jnp.einsum("in,hpn->ihp", c_conv, entering, precision=high)
    ssm = ssm + skip_gain[None, :, None] * x_conv
    gated_all = ssm.reshape(rows_here, width_here) * jax.nn.silu(z_in.astype(jnp.float32))
    halves = []
    half_rows = rows_here // 2
    for part in range(2):
        gated = gated_all[part * half_rows : (part + 1) * half_rows]
        square_sum = lax.psum(jnp.sum(gated * gated, axis=1), "tp")
        normed = (
            gated * lax.rsqrt(square_sum / DIN + epsilon)[:, None] * norm_gain[None, :]
        ).astype(jnp.bfloat16)
        mixed_cols = lax.psum_scatter(
            lax.dot_general(
                out_weight, normed, (((0,), (1,)), ((), ())), preferred_element_type=jnp.float32
            ).astype(jnp.bfloat16),
            "tp",
            scatter_dimension=0,
            tiled=True,
        )
        halves.append(mixed_cols.T)
    mixed = jnp.concatenate(halves, axis=0)
    present = holder == my_index
    inner = jnp.clip(last_row - first_row, 0, rows_here - 1)

    def finish(prompt_id, inner_row):
        return partial_at(
            device_prior, x_conv, b_conv, step_size, level, segment, inner_row, prompt_id
        )

    partials, factors_at = jax.vmap(finish)(jnp.arange(PROMPTS, dtype=jnp.int32), inner)
    partials = jnp.where(present[:, None, None, None], partials, 0.0)
    factors_at = jnp.where(present[:, None], factors_at, 0.0)

    def edge_of(inner_row, start_row, end_row):
        window = lax.dynamic_slice_in_dim(extended, inner_row + 1, KCONV - 1, 0)
        rows_global = end_row - (KCONV - 2) + jnp.arange(KCONV - 1, dtype=jnp.int32)
        return jnp.where((rows_global >= start_row)[:, None], window, jnp.zeros_like(window))

    edges = jnp.stack(
        [edge_of(inner[r], prompt_start[r], last_row[r]) for r in range(PROMPTS)]
    )
    edges = jnp.where(present[:, None, None], edges, jnp.zeros_like(edges))
    edge_cols = (KCONV - 1) * edges.shape[2]
    factor_hi = factors_at.astype(jnp.bfloat16)
    factor_lo = (factors_at - factor_hi.astype(jnp.float32)).astype(jnp.bfloat16)
    used_cols = heads_here * state_cols + edge_cols + 2 * heads_here
    slot_rows = -(-used_cols // 128)
    total_rows = PROMPTS * slot_rows
    padded_rows = -(-total_rows // (16 * seq_count)) * 16 * seq_count
    payload = jnp.concatenate(
        [
            partials.reshape(PROMPTS, heads_here * state_cols).astype(jnp.bfloat16),
            edges.reshape(PROMPTS, edge_cols),
            factor_hi,
            factor_lo,
            jnp.zeros((PROMPTS, slot_rows * 128 - used_cols), jnp.bfloat16),
        ],
        axis=1,
    ).reshape(total_rows, 128)
    payload = jnp.concatenate(
        [payload, jnp.zeros((padded_rows - total_rows, 128), jnp.bfloat16)], axis=0
    )
    summed = tree_allreduce(payload, "seq", seq_count)
    kept = summed[:total_rows].reshape(PROMPTS, slot_rows * 128)[keeper]
    factor_at = heads_here * state_cols + edge_cols
    factor_kept = kept[factor_at : factor_at + heads_here].astype(jnp.float32) + kept[
        factor_at + heads_here : factor_at + 2 * heads_here
    ].astype(jnp.float32)
    final_flat = (
        factor_kept[:, None] * entering_t
        + kept[: heads_here * state_cols].astype(jnp.float32).reshape(heads_here, state_cols)
    )
    final_state = final_flat.reshape(1, heads_here, head_width, NS)
    kept_edges = kept[heads_here * state_cols : heads_here * state_cols + edge_cols].reshape(
        KCONV - 1, edges.shape[2]
    )
    conv_edge_x = kept_edges[:, :width_here][None]
    conv_edge_bc = kept_edges[:, width_here:][None]
    return (mixed, final_state, conv_edge_x, conv_edge_bc)


def solution(mesh):
    return jax.shard_map(
        per_device,
        mesh=mesh,
        in_specs=(
            P("seq", "tp"),
            P(None, "tp"),
            P(None, "tp"),
            P(None, "tp"),
            P(None, "tp"),
            P(None, "tp"),
            P(),
            P("tp"),
            P("tp"),
            P("tp"),
            P("tp"),
            P("tp", None),
            P(),
            P("seq"),
        ),
        out_specs=(
            P("seq", "tp"),
            P("seq", "tp", None, None),
            P("seq", None, "tp"),
            P("seq", None, None),
        ),
        check_vma=False,
    )
```

```python
import jax
import jax.numpy as jnp
from jax import lax
from jax.sharding import PartitionSpec as P

NS = 128
KCONV = 4
GROUP = 256
PROMPTS = 4
DIN = 4096


highest = lax.Precision.HIGHEST
high = lax.Precision.HIGH
epsilon = 1e-05


def passed_along(block, axis, distance):
    devices = range(lax.axis_size(axis))
    route = [(i - distance, i) for i in devices if i - distance in devices]
    return lax.ppermute(block, axis, route)


def segment_of(positions, prompt_end):
    counted = jnp.sum((positions[:, None] >= prompt_end[None, :]).astype(jnp.int32), axis=1)
    return jnp.where(positions < 0, -1, counted)


def short_conv(extended, seg_ext, kernel):
    taps = kernel.shape[0]
    count = extended.shape[0] - taps + 1
    total = jnp.zeros((count, extended.shape[1]), jnp.float32)
    for offset in range(taps):
        same = (seg_ext[offset : offset + count] == seg_ext[taps - 1 :]).astype(jnp.float32)
        total = (
            total
            + extended[offset : offset + count].astype(jnp.float32)
            * kernel[offset][None, :]
            * same[:, None]
        )
    return jax.nn.silu(total).astype(jnp.bfloat16)


def advance_block(state, block):
    x_blk, b_blk, c_blk, dt_blk, log_blk, seg_blk, seg_prior = block
    length = seg_blk.shape[0]
    acum = jnp.cumsum(log_blk, axis=0)
    index = jnp.arange(length, dtype=jnp.int32)
    keep = (seg_blk[:, None] == seg_blk[None, :]) & (index[:, None] >= index[None, :])
    spread = acum[:, None, :] - acum[None, :, :]
    decay = jnp.where(keep[:, :, None], jnp.exp(jnp.where(keep[:, :, None], spread, 0.0)), 0.0)
    scores = jnp.dot(c_blk.astype(jnp.bfloat16), b_blk.T.astype(jnp.bfloat16), preferred_element_type=jnp.float32)
    mixing = scores[:, :, None] * decay * dt_blk[None, :, :]
    output = jnp.einsum("ijh,jhp->ihp", mixing, x_blk, precision=high)
    inflow = jnp.where((seg_blk == seg_prior)[:, None], jnp.exp(acum), 0.0)
    output = output + inflow[:, :, None] * jnp.einsum(
        "in,hpn->ihp", c_blk, state, precision=high
    )
    closing = seg_blk[length - 1]
    tail = (
        jnp.where((seg_blk == closing)[:, None], jnp.exp(acum[length - 1][None, :] - acum), 0.0)
        * dt_blk
    )
    fresh = jnp.einsum("jh,jhp,jn->hpn", tail, x_blk, b_blk, precision=high)
    carry = jnp.where(closing == seg_prior, jnp.exp(acum[length - 1]), 0.0)
    return carry[:, None, None] * state + fresh, output


def state_at(start_state, seg_prior, x_rows, b_rows, dt_rows, log_rows, seg_rows, inner, prompt):
    acum = jnp.cumsum(log_rows, axis=0)
    level = acum[inner]
    index = jnp.arange(seg_rows.shape[0], dtype=jnp.int32)
    chosen = (seg_rows == prompt) & (index <= inner)
    weight = (
        jnp.where(
            chosen[:, None], jnp.exp(jnp.where(chosen[:, None], level[None, :] - acum, 0.0)), 0.0
        )
        * dt_rows
    )
    inflow = jnp.where(seg_rows[inner] == seg_prior, jnp.exp(level), 0.0)
    return inflow[:, None, None] * start_state + jnp.einsum(
        "jh,jhp,jn->hpn", weight, x_rows, b_rows, precision=highest
    )


def partial_at(seg_prior, x_rows, b_rows, dt_rows, level_rows, seg_rows, inner, prompt):
    level = level_rows[inner]
    index = jnp.arange(seg_rows.shape[0], dtype=jnp.int32)
    chosen = (seg_rows == prompt) & (index <= inner)
    weight = (
        jnp.where(
            chosen[:, None],
            jnp.exp(jnp.where(chosen[:, None], level[None, :] - level_rows, 0.0)),
            0.0,
        )
        * dt_rows
    )
    inflow = jnp.where(seg_rows[inner] == seg_prior, jnp.exp(level), 0.0)
    return jnp.einsum("jh,jhp,jn->hpn", weight, x_rows, b_rows, precision=high), inflow


def tree_allreduce(big, axis, count):
    me = lax.axis_index(axis)
    order = [d for d in (1, 2, 8, 4, 16) if d < count]
    assert sorted(order) == [1 << k for k in range(count.bit_length() - 1)]
    for d in order:
        pairs = [(j, j ^ d) for j in range(count)]
        half = big.shape[0] // 2
        upper = (me // d) % 2
        send = lax.dynamic_slice_in_dim(big, (1 - upper) * half, half, 0)
        keep = lax.dynamic_slice_in_dim(big, upper * half, half, 0)
        big = keep + lax.ppermute(send, axis, pairs)
    for d in reversed(order):
        pairs = [(j, j ^ d) for j in range(count)]
        upper = (me // d) % 2 == 1
        got = lax.ppermute(big, axis, pairs)
        low = jnp.where(upper, got, big)
        high = jnp.where(upper, big, got)
        big = jnp.concatenate([low, high], axis=0)
    return big


def per_device(
    hidden,
    x_weight,
    z_weight,
    bc_weight,
    dt_weight,
    conv_x,
    conv_bc,
    dt_bias,
    decay_rate,
    skip_gain,
    norm_gain,
    out_weight,
    lengths,
    owners,
):
    rows_here = hidden.shape[0]
    width_here = x_weight.shape[1]
    heads_here = dt_bias.shape[0]
    head_width = width_here // heads_here
    seq_count = lax.axis_size("seq")
    my_index = lax.axis_index("seq")
    first_row = my_index * rows_here
    prompt_end = jnp.cumsum(lengths)
    prompt_start = prompt_end - lengths
    positions = first_row + jnp.arange(rows_here, dtype=jnp.int32)
    segment = segment_of(positions, prompt_end)
    piece = lax.all_gather(hidden, "tp", axis=1, tiled=True)
    tp_count = lax.axis_size("tp")
    tp_index = lax.axis_index("tp")
    by_shift = [bc_weight] + [
        lax.ppermute(bc_weight, "tp", [(j, (j + s) % tp_count) for j in range(tp_count)])
        for s in range(1, tp_count)
    ]
    shift_of = (tp_index - jnp.arange(tp_count, dtype=jnp.int32)) % tp_count
    bc_full = jnp.concatenate(
        [jnp.take(jnp.stack(by_shift), shift_of[k], axis=0) for k in range(tp_count)], axis=1
    )

    def take(matrix):
        return jnp.dot(piece, matrix, preferred_element_type=jnp.float32)

    x_acc = take(x_weight)
    z_acc = take(z_weight)
    dt_raw = take(dt_weight)
    bc_acc = take(bc_full)
    x_in = x_acc.astype(jnp.bfloat16)
    z_in = z_acc.astype(jnp.bfloat16)
    bc_in = bc_acc.astype(jnp.bfloat16)
    joined = jnp.concatenate([x_in, bc_in], axis=1)
    earlier = passed_along(joined[rows_here - (KCONV - 1) :], "seq", 1)
    extended = jnp.concatenate([earlier, joined], axis=0)
    seg_ext = jnp.concatenate(
        [
            segment_of(
                first_row - (KCONV - 1) + jnp.arange(KCONV - 1, dtype=jnp.int32), prompt_end
            ),
            segment,
        ]
    )
    kernel = jnp.concatenate([conv_x, conv_bc], axis=1)
    mixed_in = short_conv(extended, seg_ext, kernel)
    x_conv = mixed_in[:, :width_here].astype(jnp.float32).reshape(rows_here, heads_here, head_width)
    b_conv = mixed_in[:, width_here : width_here + NS].astype(jnp.float32)
    c_conv = mixed_in[:, width_here + NS :].astype(jnp.float32)
    step_size = jax.nn.softplus(dt_raw + dt_bias[None, :])
    log_decay = -decay_rate[None, :] * step_size
    device_prior = segment_of(jnp.reshape(first_row - 1, (1,)), prompt_end)[0]
    level = jnp.cumsum(log_decay, axis=0)
    closing = segment[rows_here - 1]
    through = jnp.where(closing == device_prior, jnp.exp(level[rows_here - 1]), 0.0)
    tail = (
        jnp.where(
            (segment == closing)[:, None], jnp.exp(level[rows_here - 1][None, :] - level), 0.0
        )
        * step_size
    )
    local_end = jnp.einsum("jh,jhp,jn->hpn", tail, x_conv, b_conv, precision=high)
    state_cols = head_width * NS
    packed_end = jnp.concatenate(
        [
            local_end.reshape(heads_here, state_cols),
            jnp.broadcast_to(through[:, None], (heads_here, 128)),
        ],
        axis=1,
    )
    gathered = lax.all_gather(packed_end, "seq")
    throughs = gathered[:, :, state_cols]
    source = jnp.arange(seq_count, dtype=jnp.int32)
    last_row = prompt_end - 1
    holder = last_row // rows_here
    keeper = owners[0]

    def entering_of(target):
        between = (source[None, :] > source[:, None]) & (source[None, :] < target)
        factors = jnp.where(between[:, :, None], throughs[None, :, :], 1.0)
        weights = jnp.where((source < target)[:, None], jnp.prod(factors, axis=1), 0.0)
        return jnp.sum(weights[:, :, None] * gathered[:, :, :state_cols], axis=0)

    entering = entering_of(my_index).reshape(heads_here, head_width, NS)
    entering_t = entering_of(holder[keeper])

    blocks = rows_here // GROUP
    state = jnp.zeros((heads_here, head_width, NS), jnp.float32)
    pieces = []
    for blk in range(blocks):
        rows = slice(blk * GROUP, (blk + 1) * GROUP)
        seg_prior = device_prior if blk == 0 else segment[blk * GROUP - 1]
        state, output = advance_block(
            state,
            (
                x_conv[rows],
                b_conv[rows],
                c_conv[rows],
                step_size[rows],
                log_decay[rows],
                segment[rows],
                seg_prior,
            ),
        )
        pieces.append(output)
    ssm = jnp.concatenate(pieces, axis=0)
    inflow = jnp.where((segment == device_prior)[:, None], jnp.exp(level), 0.0)
    ssm = ssm + inflow[:, :, None] * jnp.einsum("in,hpn->ihp", c_conv, entering, precision=high)
    ssm = ssm + skip_gain[None, :, None] * x_conv
    gated_all = ssm.reshape(rows_here, width_here) * jax.nn.silu(z_in.astype(jnp.float32))
    halves = []
    half_rows = rows_here
    for part in range(1):
        gated = gated_all[part * half_rows : (part + 1) * half_rows]
        square_sum = lax.psum(jnp.sum(gated * gated, axis=1), "tp")
        normed = (
            gated * lax.rsqrt(square_sum / DIN + epsilon)[:, None] * norm_gain[None, :]
        ).astype(jnp.bfloat16)
        mixed_cols = lax.psum_scatter(
            lax.dot_general(
                out_weight, normed, (((0,), (1,)), ((), ())), preferred_element_type=jnp.float32
            ).astype(jnp.bfloat16),
            "tp",
            scatter_dimension=0,
            tiled=True,
        )
        halves.append(mixed_cols.T)
    mixed = jnp.concatenate(halves, axis=0)
    present = holder == my_index
    inner = jnp.clip(last_row - first_row, 0, rows_here - 1)

    def finish(prompt_id, inner_row):
        return partial_at(
            device_prior, x_conv, b_conv, step_size, level, segment, inner_row, prompt_id
        )

    partials, factors_at = jax.vmap(finish)(jnp.arange(PROMPTS, dtype=jnp.int32), inner)
    partials = jnp.where(present[:, None, None, None], partials, 0.0)
    factors_at = jnp.where(present[:, None], factors_at, 0.0)

    def edge_of(inner_row, start_row, end_row):
        window = lax.dynamic_slice_in_dim(extended, inner_row + 1, KCONV - 1, 0)
        rows_global = end_row - (KCONV - 2) + jnp.arange(KCONV - 1, dtype=jnp.int32)
        return jnp.where((rows_global >= start_row)[:, None], window, jnp.zeros_like(window))

    edges = jnp.stack(
        [edge_of(inner[r], prompt_start[r], last_row[r]) for r in range(PROMPTS)]
    )
    edges = jnp.where(present[:, None, None], edges, jnp.zeros_like(edges))
    edge_cols = (KCONV - 1) * edges.shape[2]
    factor_hi = factors_at.astype(jnp.bfloat16)
    factor_lo = (factors_at - factor_hi.astype(jnp.float32)).astype(jnp.bfloat16)
    used_cols = heads_here * state_cols + edge_cols + 2 * heads_here
    slot_rows = -(-used_cols // 128)
    total_rows = PROMPTS * slot_rows
    padded_rows = -(-total_rows // (16 * seq_count)) * 16 * seq_count
    payload = jnp.concatenate(
        [
            partials.reshape(PROMPTS, heads_here * state_cols).astype(jnp.bfloat16),
            edges.reshape(PROMPTS, edge_cols),
            factor_hi,
            factor_lo,
            jnp.zeros((PROMPTS, slot_rows * 128 - used_cols), jnp.bfloat16),
        ],
        axis=1,
    ).reshape(total_rows, 128)
    payload = jnp.concatenate(
        [payload, jnp.zeros((padded_rows - total_rows, 128), jnp.bfloat16)], axis=0
    )
    summed = tree_allreduce(payload, "seq", seq_count)
    kept = summed[:total_rows].reshape(PROMPTS, slot_rows * 128)[keeper]
    factor_at = heads_here * state_cols + edge_cols
    factor_kept = kept[factor_at : factor_at + heads_here].astype(jnp.float32) + kept[
        factor_at + heads_here : factor_at + 2 * heads_here
    ].astype(jnp.float32)
    final_flat = (
        factor_kept[:, None] * entering_t
        + kept[: heads_here * state_cols].astype(jnp.float32).reshape(heads_here, state_cols)
    )
    final_state = final_flat.reshape(1, heads_here, head_width, NS)
    kept_edges = kept[heads_here * state_cols : heads_here * state_cols + edge_cols].reshape(
        KCONV - 1, edges.shape[2]
    )
    conv_edge_x = kept_edges[:, :width_here][None]
    conv_edge_bc = kept_edges[:, width_here:][None]
    return (mixed, final_state, conv_edge_x, conv_edge_bc)


def solution(mesh):
    return jax.shard_map(
        per_device,
        mesh=mesh,
        in_specs=(
            P("seq", "tp"),
            P(None, "tp"),
            P(None, "tp"),
            P(None, "tp"),
            P(None, "tp"),
            P(None, "tp"),
            P(),
            P("tp"),
            P("tp"),
            P("tp"),
            P("tp"),
            P("tp", None),
            P(),
            P("seq"),
        ),
        out_specs=(
            P("seq", "tp"),
            P("seq", "tp", None, None),
            P("seq", None, "tp"),
            P("seq", None, None),
        ),
        check_vma=False,
    )
```

```python
import jax
import jax.numpy as jnp
from jax import lax
from jax.sharding import PartitionSpec as P

NS = 128
KCONV = 4
GROUP = 256
PROMPTS = 4
DIN = 4096


highest = lax.Precision.HIGHEST
high = lax.Precision.HIGH
epsilon = 1e-05


def passed_along(block, axis, distance):
    devices = range(lax.axis_size(axis))
    route = [(i - distance, i) for i in devices if i - distance in devices]
    return lax.ppermute(block, axis, route)


def segment_of(positions, prompt_end):
    counted = jnp.sum((positions[:, None] >= prompt_end[None, :]).astype(jnp.int32), axis=1)
    return jnp.where(positions < 0, -1, counted)


def short_conv(extended, seg_ext, kernel):
    taps = kernel.shape[0]
    count = extended.shape[0] - taps + 1
    total = jnp.zeros((count, extended.shape[1]), jnp.float32)
    for offset in range(taps):
        same = (seg_ext[offset : offset + count] == seg_ext[taps - 1 :]).astype(jnp.float32)
        total = (
            total
            + extended[offset : offset + count].astype(jnp.float32)
            * kernel[offset][None, :]
            * same[:, None]
        )
    return jax.nn.silu(total).astype(jnp.bfloat16)


def advance_block(state, block):
    x_blk, b_blk, c_blk, dt_blk, log_blk, seg_blk, seg_prior = block
    length = seg_blk.shape[0]
    acum = jnp.cumsum(log_blk, axis=0)
    index = jnp.arange(length, dtype=jnp.int32)
    keep = (seg_blk[:, None] == seg_blk[None, :]) & (index[:, None] >= index[None, :])
    spread = acum[:, None, :] - acum[None, :, :]
    decay = jnp.where(keep[:, :, None], jnp.exp(jnp.where(keep[:, :, None], spread, 0.0)), 0.0)
    scores = jnp.dot(c_blk.astype(jnp.bfloat16), b_blk.T.astype(jnp.bfloat16), preferred_element_type=jnp.float32)
    mixing = scores[:, :, None] * decay * dt_blk[None, :, :]
    output = jnp.einsum("ijh,jhp->ihp", mixing, x_blk, precision=high)
    inflow = jnp.where((seg_blk == seg_prior)[:, None], jnp.exp(acum), 0.0)
    output = output + inflow[:, :, None] * jnp.einsum(
        "in,hpn->ihp", c_blk, state, precision=high
    )
    closing = seg_blk[length - 1]
    tail = (
        jnp.where((seg_blk == closing)[:, None], jnp.exp(acum[length - 1][None, :] - acum), 0.0)
        * dt_blk
    )
    fresh = jnp.einsum("jh,jhp,jn->hpn", tail, x_blk, b_blk, precision=high)
    carry = jnp.where(closing == seg_prior, jnp.exp(acum[length - 1]), 0.0)
    return carry[:, None, None] * state + fresh, output


def state_at(start_state, seg_prior, x_rows, b_rows, dt_rows, log_rows, seg_rows, inner, prompt):
    acum = jnp.cumsum(log_rows, axis=0)
    level = acum[inner]
    index = jnp.arange(seg_rows.shape[0], dtype=jnp.int32)
    chosen = (seg_rows == prompt) & (index <= inner)
    weight = (
        jnp.where(
            chosen[:, None], jnp.exp(jnp.where(chosen[:, None], level[None, :] - acum, 0.0)), 0.0
        )
        * dt_rows
    )
    inflow = jnp.where(seg_rows[inner] == seg_prior, jnp.exp(level), 0.0)
    return inflow[:, None, None] * start_state + jnp.einsum(
        "jh,jhp,jn->hpn", weight, x_rows, b_rows, precision=highest
    )


def partial_at(seg_prior, x_rows, b_rows, dt_rows, level_rows, seg_rows, inner, prompt):
    level = level_rows[inner]
    index = jnp.arange(seg_rows.shape[0], dtype=jnp.int32)
    chosen = (seg_rows == prompt) & (index <= inner)
    weight = (
        jnp.where(
            chosen[:, None],
            jnp.exp(jnp.where(chosen[:, None], level[None, :] - level_rows, 0.0)),
            0.0,
        )
        * dt_rows
    )
    inflow = jnp.where(seg_rows[inner] == seg_prior, jnp.exp(level), 0.0)
    return jnp.einsum("jh,jhp,jn->hpn", weight, x_rows, b_rows, precision=high), inflow


def tree_allreduce(big, axis, count):
    me = lax.axis_index(axis)
    order = [d for d in (1, 2, 8, 4, 16) if d < count]
    assert sorted(order) == [1 << k for k in range(count.bit_length() - 1)]
    for d in order:
        pairs = [(j, j ^ d) for j in range(count)]
        half = big.shape[0] // 2
        upper = (me // d) % 2
        send = lax.dynamic_slice_in_dim(big, (1 - upper) * half, half, 0)
        keep = lax.dynamic_slice_in_dim(big, upper * half, half, 0)
        big = keep + lax.ppermute(send, axis, pairs)
    for d in reversed(order):
        pairs = [(j, j ^ d) for j in range(count)]
        upper = (me // d) % 2 == 1
        got = lax.ppermute(big, axis, pairs)
        low = jnp.where(upper, got, big)
        high = jnp.where(upper, big, got)
        big = jnp.concatenate([low, high], axis=0)
    return big


def per_device(
    hidden,
    x_weight,
    z_weight,
    bc_weight,
    dt_weight,
    conv_x,
    conv_bc,
    dt_bias,
    decay_rate,
    skip_gain,
    norm_gain,
    out_weight,
    lengths,
    owners,
):
    rows_here = hidden.shape[0]
    width_here = x_weight.shape[1]
    heads_here = dt_bias.shape[0]
    head_width = width_here // heads_here
    seq_count = lax.axis_size("seq")
    my_index = lax.axis_index("seq")
    first_row = my_index * rows_here
    prompt_end = jnp.cumsum(lengths)
    prompt_start = prompt_end - lengths
    positions = first_row + jnp.arange(rows_here, dtype=jnp.int32)
    segment = segment_of(positions, prompt_end)
    piece = lax.all_gather(hidden, "tp", axis=1, tiled=True)
    tp_count = lax.axis_size("tp")
    tp_index = lax.axis_index("tp")
    by_shift = [bc_weight] + [
        lax.ppermute(bc_weight, "tp", [(j, (j + s) % tp_count) for j in range(tp_count)])
        for s in range(1, tp_count)
    ]
    shift_of = (tp_index - jnp.arange(tp_count, dtype=jnp.int32)) % tp_count
    bc_full = jnp.concatenate(
        [jnp.take(jnp.stack(by_shift), shift_of[k], axis=0) for k in range(tp_count)], axis=1
    )

    def take(matrix):
        return jnp.dot(piece, matrix, preferred_element_type=jnp.float32)

    x_acc = take(x_weight)
    z_acc = take(z_weight)
    dt_raw = take(dt_weight)
    bc_acc = take(bc_full)
    x_in = x_acc.astype(jnp.bfloat16)
    z_in = z_acc.astype(jnp.bfloat16)
    bc_in = bc_acc.astype(jnp.bfloat16)
    joined = jnp.concatenate([x_in, bc_in], axis=1)
    earlier = passed_along(joined[rows_here - (KCONV - 1) :], "seq", 1)
    extended = jnp.concatenate([earlier, joined], axis=0)
    seg_ext = jnp.concatenate(
        [
            segment_of(
                first_row - (KCONV - 1) + jnp.arange(KCONV - 1, dtype=jnp.int32), prompt_end
            ),
            segment,
        ]
    )
    kernel = jnp.concatenate([conv_x, conv_bc], axis=1)
    mixed_in = short_conv(extended, seg_ext, kernel)
    x_conv = mixed_in[:, :width_here].astype(jnp.float32).reshape(rows_here, heads_here, head_width)
    b_conv = mixed_in[:, width_here : width_here + NS].astype(jnp.float32)
    c_conv = mixed_in[:, width_here + NS :].astype(jnp.float32)
    step_size = jax.nn.softplus(dt_raw + dt_bias[None, :])
    log_decay = -decay_rate[None, :] * step_size
    device_prior = segment_of(jnp.reshape(first_row - 1, (1,)), prompt_end)[0]
    row_ids = jnp.arange(rows_here, dtype=jnp.int32)
    lower = (row_ids[:, None] >= row_ids[None, :]).astype(jnp.float32)
    level = jnp.dot(lower, log_decay, precision=highest)
    closing = segment[rows_here - 1]
    through = jnp.where(closing == device_prior, jnp.exp(level[rows_here - 1]), 0.0)
    tail = (
        jnp.where(
            (segment == closing)[:, None], jnp.exp(level[rows_here - 1][None, :] - level), 0.0
        )
        * step_size
    )
    local_end = jnp.einsum("jh,jhp,jn->hpn", tail, x_conv, b_conv, precision=high)
    state_cols = head_width * NS
    packed_end = jnp.concatenate(
        [
            local_end.reshape(heads_here, state_cols),
            jnp.broadcast_to(through[:, None], (heads_here, 128)),
        ],
        axis=1,
    )
    gathered = lax.all_gather(packed_end, "seq")
    throughs = gathered[:, :, state_cols]
    source = jnp.arange(seq_count, dtype=jnp.int32)
    last_row = prompt_end - 1
    holder = last_row // rows_here
    keeper = owners[0]

    def entering_of(target):
        between = (source[None, :] > source[:, None]) & (source[None, :] < target)
        factors = jnp.where(between[:, :, None], throughs[None, :, :], 1.0)
        weights = jnp.where((source < target)[:, None], jnp.prod(factors, axis=1), 0.0)
        return jnp.sum(weights[:, :, None] * gathered[:, :, :state_cols], axis=0)

    entering = entering_of(my_index).reshape(heads_here, head_width, NS)
    entering_t = entering_of(holder[keeper])

    blocks = rows_here // GROUP
    state = jnp.zeros((heads_here, head_width, NS), jnp.float32)
    pieces = []
    for blk in range(blocks):
        rows = slice(blk * GROUP, (blk + 1) * GROUP)
        seg_prior = device_prior if blk == 0 else segment[blk * GROUP - 1]
        state, output = advance_block(
            state,
            (
                x_conv[rows],
                b_conv[rows],
                c_conv[rows],
                step_size[rows],
                log_decay[rows],
                segment[rows],
                seg_prior,
            ),
        )
        pieces.append(output)
    ssm = jnp.concatenate(pieces, axis=0)
    inflow = jnp.where((segment == device_prior)[:, None], jnp.exp(level), 0.0)
    ssm = ssm + inflow[:, :, None] * jnp.einsum("in,hpn->ihp", c_conv, entering, precision=high)
    ssm = ssm + skip_gain[None, :, None] * x_conv
    gated_all = ssm.reshape(rows_here, width_here) * jax.nn.silu(z_in.astype(jnp.float32))
    halves = []
    half_rows = rows_here // 2
    for part in range(2):
        gated = gated_all[part * half_rows : (part + 1) * half_rows]
        square_sum = lax.psum(jnp.sum(gated * gated, axis=1), "tp")
        normed = (
            gated * lax.rsqrt(square_sum / DIN + epsilon)[:, None] * norm_gain[None, :]
        ).astype(jnp.bfloat16)
        mixed_cols = lax.psum_scatter(
            lax.dot_general(
                out_weight, normed, (((0,), (1,)), ((), ())), preferred_element_type=jnp.float32
            ).astype(jnp.bfloat16),
            "tp",
            scatter_dimension=0,
            tiled=True,
        )
        halves.append(mixed_cols.T)
    mixed = jnp.concatenate(halves, axis=0)
    present = holder == my_index
    inner = jnp.clip(last_row - first_row, 0, rows_here - 1)

    def finish(prompt_id, inner_row):
        return partial_at(
            device_prior, x_conv, b_conv, step_size, level, segment, inner_row, prompt_id
        )

    partials, factors_at = jax.vmap(finish)(jnp.arange(PROMPTS, dtype=jnp.int32), inner)
    partials = jnp.where(present[:, None, None, None], partials, 0.0)
    factors_at = jnp.where(present[:, None], factors_at, 0.0)

    def edge_of(inner_row, start_row, end_row):
        window = lax.dynamic_slice_in_dim(extended, inner_row + 1, KCONV - 1, 0)
        rows_global = end_row - (KCONV - 2) + jnp.arange(KCONV - 1, dtype=jnp.int32)
        return jnp.where((rows_global >= start_row)[:, None], window, jnp.zeros_like(window))

    edges = jnp.stack(
        [edge_of(inner[r], prompt_start[r], last_row[r]) for r in range(PROMPTS)]
    )
    edges = jnp.where(present[:, None, None], edges, jnp.zeros_like(edges))
    edge_cols = (KCONV - 1) * edges.shape[2]
    factor_hi = factors_at.astype(jnp.bfloat16)
    factor_lo = (factors_at - factor_hi.astype(jnp.float32)).astype(jnp.bfloat16)
    used_cols = heads_here * state_cols + edge_cols + 2 * heads_here
    slot_rows = -(-used_cols // 128)
    total_rows = PROMPTS * slot_rows
    padded_rows = -(-total_rows // (16 * seq_count)) * 16 * seq_count
    payload = jnp.concatenate(
        [
            partials.reshape(PROMPTS, heads_here * state_cols).astype(jnp.bfloat16),
            edges.reshape(PROMPTS, edge_cols),
            factor_hi,
            factor_lo,
            jnp.zeros((PROMPTS, slot_rows * 128 - used_cols), jnp.bfloat16),
        ],
        axis=1,
    ).reshape(total_rows, 128)
    payload = jnp.concatenate(
        [payload, jnp.zeros((padded_rows - total_rows, 128), jnp.bfloat16)], axis=0
    )
    summed = tree_allreduce(payload, "seq", seq_count)
    kept = summed[:total_rows].reshape(PROMPTS, slot_rows * 128)[keeper]
    factor_at = heads_here * state_cols + edge_cols
    factor_kept = kept[factor_at : factor_at + heads_here].astype(jnp.float32) + kept[
        factor_at + heads_here : factor_at + 2 * heads_here
    ].astype(jnp.float32)
    final_flat = (
        factor_kept[:, None] * entering_t
        + kept[: heads_here * state_cols].astype(jnp.float32).reshape(heads_here, state_cols)
    )
    final_state = final_flat.reshape(1, heads_here, head_width, NS)
    kept_edges = kept[heads_here * state_cols : heads_here * state_cols + edge_cols].reshape(
        KCONV - 1, edges.shape[2]
    )
    conv_edge_x = kept_edges[:, :width_here][None]
    conv_edge_bc = kept_edges[:, width_here:][None]
    return (mixed, final_state, conv_edge_x, conv_edge_bc)


def solution(mesh):
    return jax.shard_map(
        per_device,
        mesh=mesh,
        in_specs=(
            P("seq", "tp"),
            P(None, "tp"),
            P(None, "tp"),
            P(None, "tp"),
            P(None, "tp"),
            P(None, "tp"),
            P(),
            P("tp"),
            P("tp"),
            P("tp"),
            P("tp"),
            P("tp", None),
            P(),
            P("seq"),
        ),
        out_specs=(
            P("seq", "tp"),
            P("seq", "tp", None, None),
            P("seq", None, "tp"),
            P("seq", None, None),
        ),
        check_vma=False,
    )
```
